128 devices in a mesh: grp: 4 (over z), shard: 32 (over y, x, core).
Axes of the slice: x: 4, y: 4, z: 4, core: 2. Of those that a mesh axis runs over, the one named last changes fastest.
Arguments:
- users: float32 [65536, 128], P(('grp', 'shard')), may hold values from -2 to 2
- user_accum: float32 [65536, 128], P(('grp', 'shard')), may hold values from 100 to 3000
- positives: int32 [65536, 16], P(('grp', 'shard')), may hold values from 0 to 32767
- hot_table: float32 [32768, 128], P('shard'), may hold values from -2 to 2
- hot_accum: float32 [32768, 128], P('shard'), may hold values from 100 to 3000
- cold_table: float32 [131072, 128], P(('grp', 'shard')), may hold values from -2 to 2
- cold_accum: float32 [131072, 128], P(('grp', 'shard')), may hold values from 4 to 100
- cold_requests: int32 [128, 128, 128], P(('grp', 'shard')), may hold values from 0 to 1023
- cold_counts: int32 [128, 128], P(('grp', 'shard')), may hold values from 1 to 128, as said below
Outputs:
- new_users: float32 [65536, 128], P(('grp', 'shard'))
- new_user_accum: float32 [65536, 128], P(('grp', 'shard'))
- new_hot: float32 [32768, 128], P('shard')
- new_hot_accum: float32 [32768, 128], P('shard')
- new_cold: float32 [131072, 128], P(('grp', 'shard'))
- new_cold_accum: float32 [131072, 128], P(('grp', 'shard'))
The draws below stay inside these ranges and needn't reach their ends.
Inputs may be any that keep to these rules, and one draw needn't show every extreme that they name: Slots s < cold_counts[d, o] of block (d, o) are live, the rest are padding. Every device has an owner of which it asks 128 live rows, and in every draw one owner receives 128 live rows from every device.
All inputs are finite; a program needn't handle non-finite values.
Results may differ from the reference program's by a relative error of at most 0.0089.
Values may be sent and summed in bfloat16 or wider, within the bound.
No kernel may reach another device: no remote copies, remote signals or barrier semaphores. Data moves between devices by JAX's collectives and lax.ppermute only.
A program may use at most 192 MiB of HBM per device.

```python
import math
import jax
import jax.numpy as jnp
from jax import lax

K = 128
COLD_DEV = 1024
CAP = 128
POS = 16
USERS = 65536
HOT = 32768
COLD = 131072
DEVICES = 128


def draw_cold_counts(key, part):
    streams = jax.random.split(jax.random.fold_in(key, 11), 4)
    owner_weight = jax.random.randint(streams[0], (1, DEVICES), 1, 5)
    spread_draw = jax.random.randint(streams[1], (DEVICES, DEVICES), CAP // 16, CAP // 4 + 1)
    counts = jnp.minimum(owner_weight * spread_draw, CAP)
    partner = jax.random.randint(streams[2], (DEVICES, 1), 0, DEVICES)
    crowded = jax.random.randint(streams[3], (), 0, DEVICES)
    column = lax.iota(jnp.int32, DEVICES)[None, :]
    filled = (column == partner) | (column == crowded)
    return jnp.where(filled, CAP, counts).astype(jnp.int32)


def plant(entries, key, low, top_value):
    spot = [jax.random.randint(jax.random.fold_in(key, axis), (), 0, length) for axis, length in enumerate(entries.shape)]
    longest = entries.shape.index(max(entries.shape))
    beside = spot[:longest] + [(spot[longest] + 1) % entries.shape[longest]] + spot[longest + 1:]
    return entries.at[tuple(spot)].set(low).at[tuple(beside)].set(top_value)


def block_levels(stream_key, dims, pieces, low, top_value):
    def one(position, parts):
        steps = jax.random.uniform(jax.random.fold_in(jax.random.fold_in(stream_key, 6), position), (parts,), jnp.float32, low / len(pieces), top_value / len(pieces))
        return jnp.repeat(jnp.exp(steps), dims[position] // parts).reshape((-1,) + (1,) * (len(dims) - position - 1))

    loudness = one(*pieces[0])
    for cut in pieces[1:]:
        loudness = loudness * one(*cut)
    return loudness


def gaussian(stream_key, shape, deviation, limit, pieces=(), dtype=jnp.bfloat16):
    drawn = deviation * jax.random.normal(stream_key, shape, jnp.float32)
    if pieces:
        drawn = drawn * block_levels(stream_key, shape, pieces, -0.22, 0.18)
    return jnp.clip(drawn, -limit, limit).astype(dtype)


def setup_inputs(seed: int = 0) -> dict:
    streams_of = jax.random.split(jax.random.key(seed), 10)
    users = gaussian(streams_of[0], (USERS, K), 0.3, 2.0, ((0, 128),), jnp.float32)
    user_accum = jnp.clip(jnp.exp(math.log(3000.0) - 3.4011974 * jax.random.uniform(streams_of[1], (USERS, K), jnp.float32) ** block_levels(streams_of[1], (USERS, K), ((0, 128),), -0.2, 0.2)), 100.0, 3000.0)
    positives = plant(jax.random.randint(streams_of[2], (USERS, POS), 0, HOT), jax.random.fold_in(streams_of[2], 1), 0, HOT - 1).astype(jnp.int32)
    hot_table = gaussian(streams_of[3], (HOT, K), 0.3, 2.0, ((0, 32),), jnp.float32)
    hot_accum = jnp.clip(jnp.exp(math.log(3000.0) - 3.4011974 * jax.random.uniform(streams_of[4], (HOT, K), jnp.float32) ** block_levels(streams_of[4], (HOT, K), ((0, 32),), -0.2, 0.2)), 100.0, 3000.0)
    cold_table = gaussian(streams_of[5], (COLD, K), 0.3, 2.0, ((0, 128),), jnp.float32)
    cold_accum = jnp.clip(jnp.exp(math.log(100.0) - 3.218876 * jax.random.uniform(streams_of[6], (COLD, K), jnp.float32) ** block_levels(streams_of[6], (COLD, K), ((0, 128),), -0.2, 0.2)), 4.0, 100.0)
    cold_requests = plant(jax.random.randint(streams_of[7], (DEVICES, DEVICES, CAP), 0, COLD_DEV), jax.random.fold_in(streams_of[7], 1), 0, COLD_DEV - 1).astype(jnp.int32)
    cold_counts = draw_cold_counts(jax.random.fold_in(streams_of[9], 71), 0)
    return {"users": users, "user_accum": user_accum, "positives": positives, "hot_table": hot_table, "hot_accum": hot_accum, "cold_table": cold_table, "cold_accum": cold_accum, "cold_requests": cold_requests, "cold_counts": cold_counts}


POSITIVE_WEIGHT = 32.0
LEARN_RATE = 0.5

def hot_block(user_rows, pos_rows, item_rows, item_first):
    item_ids = item_first + lax.iota(jnp.int32, item_rows.shape[0])
    matches = lax.optimization_barrier(jnp.sum((pos_rows[:, :, None] == item_ids[None, None, :]).astype(jnp.float32), axis=1))
    scores = jnp.dot(user_rows, item_rows.T, preferred_element_type=jnp.float32)
    weights = ((1.0 + POSITIVE_WEIGHT * matches) * jax.nn.sigmoid(scores) - POSITIVE_WEIGHT * matches).astype(jnp.bfloat16)
    user_part = jnp.dot(weights, item_rows, preferred_element_type=jnp.float32)
    item_part = jnp.dot(weights.T, user_rows, preferred_element_type=jnp.float32)
    return (user_part, item_part)

def adagrad(current, history, gradient):
    updated = history + gradient * gradient
    return (current - LEARN_RATE * gradient / jnp.sqrt(updated), updated)

def reference(users, user_accum, positives, hot_table, hot_accum, cold_table, cold_accum, cold_requests, cold_counts):
    user_half = users.astype(jnp.bfloat16)
    hot_half = hot_table.astype(jnp.bfloat16)
    cold_half = cold_table.astype(jnp.bfloat16)
    devices = cold_requests.shape[0]
    slot_count = cold_requests.shape[2]
    feature_count = users.shape[1]
    per_device = users.shape[0] // devices
    owner_rows = cold_table.shape[0] // devices
    offsets = lax.iota(jnp.int32, devices) * owner_rows

    def step(state_pair, inputs):
        hot_grad, cold_grad = state_pair
        user_rows, pos_rows, requests, counts = inputs
        user_hot, item_part = hot_block(user_rows, pos_rows, hot_half, jnp.int32(0))
        global_rows = (offsets[:, None] + requests.astype(jnp.int32)).reshape(-1).astype(jnp.int32)
        flat_rows = jnp.take(cold_half, global_rows, axis=0)
        live_slots = (lax.iota(jnp.int32, slot_count)[None, :] < counts[:, None]).reshape(-1)
        scores = jnp.dot(user_rows, flat_rows.T, preferred_element_type=jnp.float32)
        weights = (jax.nn.sigmoid(scores) * live_slots[None, :].astype(jnp.float32)).astype(jnp.bfloat16)
        user_cold = jnp.dot(weights, flat_rows, preferred_element_type=jnp.float32)
        row_terms = jnp.dot(weights.T, user_rows, preferred_element_type=jnp.float32).astype(jnp.bfloat16)
        cold_grad = cold_grad.at[global_rows].add(row_terms.astype(jnp.float32))
        return ((hot_grad + item_part, cold_grad), user_hot + user_cold)
    initial = (jnp.zeros(hot_table.shape, jnp.float32), jnp.zeros(cold_table.shape, jnp.float32))
    inputs = (user_half.reshape(devices, per_device, feature_count), positives.reshape(devices, per_device, positives.shape[1]), cold_requests, cold_counts)
    (hot_grad, cold_grad), user_grad = lax.scan(step, initial, inputs)
    user_grad = user_grad.reshape(-1, feature_count)
    new_users, new_user_accum = adagrad(users, user_accum, user_grad)
    new_hot, new_hot_accum = adagrad(hot_table, hot_accum, hot_grad)
    new_cold, new_cold_accum = adagrad(cold_table, cold_accum, cold_grad)
    return (new_users, new_user_accum, new_hot, new_hot_accum, new_cold, new_cold_accum)
```

```python
import functools

import jax
import jax.numpy as jnp
from jax import lax
from jax.experimental import pallas as pl
from jax.experimental.pallas import tpu as pltpu
from jax.sharding import PartitionSpec as P

POSITIVE_WEIGHT = 32.0
LEARN_RATE = 0.5
LANES = 128
SUB = 8


def _nt(a, b):
    return lax.dot_general(a, b, (((1,), (1,)), ((), ())), preferred_element_type=jnp.float32)


def _tn(a, b):
    return lax.dot_general(a, b, (((0,), (0,)), ((), ())), preferred_element_type=jnp.float32)


def _hot_kernel(u_ref, h_ref, ph_ref, ol_ref, up_ref, ip_ref, m_ref):
    j = pl.program_id(0)
    block = h_ref.shape[0]
    nh = block // LANES
    subtiles = ph_ref.shape[0]
    per = LANES // SUB
    r = lax.broadcasted_iota(jnp.int32, (nh * SUB, LANES), 0)
    c = lax.broadcasted_iota(jnp.int32, (nh * SUB, LANES), 1)
    diag = (r % SUB) == (c // per)
    hrow = r // SUB + j * nh

    def sub(s, carry):
        ph = ph_ref[pl.ds(s, 1), :]
        lhs = jnp.where(diag & (ph == hrow), 1.0, 0.0).astype(jnp.bfloat16)
        out = _nt(lhs, ol_ref[s])
        base = pl.multiple_of(s * SUB, SUB)
        for h in range(nh):
            m_ref[pl.ds(base, SUB), pl.ds(h * LANES, LANES)] = out[h * SUB:(h + 1) * SUB, :]
        return carry

    lax.fori_loop(0, subtiles, sub, 0)
    u = u_ref[...]
    hj = h_ref[...]
    scores = _nt(u, hj)
    m = m_ref[...]
    w = ((1.0 + POSITIVE_WEIGHT * m) * jax.nn.sigmoid(scores) - POSITIVE_WEIGHT * m).astype(
        jnp.bfloat16
    )

    @pl.when(j == 0)
    def _():
        up_ref[...] = jnp.zeros_like(up_ref)

    up_ref[...] += jnp.dot(w, hj, preferred_element_type=jnp.float32)
    ip_ref[...] = _tn(w, u)


def hot_terms(user_half, positives, hot_all, block=2048):
    users, k = user_half.shape
    items = hot_all.shape[0]
    pos_count = positives.shape[1]
    subtiles = users // SUB
    assert SUB * pos_count == LANES
    pos_hi = (positives // LANES).reshape(subtiles, LANES)
    pos_lo = (positives % LANES).reshape(subtiles, 1, LANES)
    onehot_lo = (pos_lo == lax.broadcasted_iota(jnp.int32, (1, LANES, 1), 1)).astype(jnp.bfloat16)
    return pl.pallas_call(
        _hot_kernel,
        grid=(items // block,),
        in_specs=[
            pl.BlockSpec((users, k), lambda j: (0, 0)),
            pl.BlockSpec((block, k), lambda j: (j, 0)),
            pl.BlockSpec((subtiles, LANES), lambda j: (0, 0)),
            pl.BlockSpec((subtiles, LANES, LANES), lambda j: (0, 0, 0)),
        ],
        out_specs=[
            pl.BlockSpec((users, k), lambda j: (0, 0)),
            pl.BlockSpec((block, k), lambda j: (j, 0)),
        ],
        out_shape=[
            jax.ShapeDtypeStruct((users, k), jnp.float32),
            jax.ShapeDtypeStruct((items, k), jnp.float32),
        ],
        scratch_shapes=[pltpu.VMEM((users, block), jnp.float32)],
        compiler_params=pltpu.CompilerParams(dimension_semantics=("arbitrary",)),
    )(user_half, hot_all, pos_hi, onehot_lo)


def _gather_kernel(idx_ref, table_ref, out_ref):
    rows = table_ref.shape[0]
    onehot = (idx_ref[...] == lax.broadcasted_iota(jnp.int32, (1, rows), 1)).astype(jnp.bfloat16)
    out_ref[...] = jnp.dot(onehot, table_ref[...], preferred_element_type=jnp.float32).astype(
        out_ref.dtype
    )


def onehot_gather(table, idx, chunk=1024):
    rows, k = table.shape
    n = idx.shape[0]
    return pl.pallas_call(
        _gather_kernel,
        grid=(n // chunk,),
        in_specs=[
            pl.BlockSpec((chunk, 1), lambda i: (i, 0)),
            pl.BlockSpec((rows, k), lambda i: (0, 0)),
        ],
        out_specs=pl.BlockSpec((chunk, k), lambda i: (i, 0)),
        out_shape=jax.ShapeDtypeStruct((n, k), table.dtype),
    )(idx.reshape(n, 1), table)


def _scatter_kernel(idx_ref, val_ref, out_ref):
    i = pl.program_id(0)
    rows = out_ref.shape[0]
    chunk = idx_ref.shape[1]
    onehot = (idx_ref[...] == lax.broadcasted_iota(jnp.int32, (rows, chunk), 0)).astype(
        jnp.bfloat16
    )

    @pl.when(i == 0)
    def _():
        out_ref[...] = jnp.zeros_like(out_ref)

    out_ref[...] += jnp.dot(onehot, val_ref[...], preferred_element_type=jnp.float32)


def onehot_scatter_add(idx, values, rows, chunk=1024):
    n, k = values.shape
    return pl.pallas_call(
        _scatter_kernel,
        grid=(n // chunk,),
        in_specs=[
            pl.BlockSpec((1, chunk), lambda i: (0, i)),
            pl.BlockSpec((chunk, k), lambda i: (i, 0)),
        ],
        out_specs=pl.BlockSpec((rows, k), lambda i: (0, 0)),
        out_shape=jax.ShapeDtypeStruct((rows, k), jnp.float32),
        compiler_params=pltpu.CompilerParams(dimension_semantics=("arbitrary",)),
    )(idx.reshape(1, n), values)


def adagrad(current, history, gradient):
    updated = history + gradient * gradient
    return (current - LEARN_RATE * gradient / jnp.sqrt(updated), updated)


def body(
    users,
    user_accum,
    positives,
    hot_table,
    hot_accum,
    cold_table,
    cold_accum,
    cold_requests,
    cold_counts,
):
    user_half = users.astype(jnp.bfloat16)
    hot_half = hot_table.astype(jnp.bfloat16)
    cold_half = cold_table.astype(jnp.bfloat16)
    feature_count = users.shape[1]
    hot_all = lax.all_gather(hot_half, "shard", axis=0, tiled=True)
    item_total = hot_all.shape[0]
    user_hot, item_parts = hot_terms(user_half, positives, hot_all)
    item_grad = lax.psum_scatter(item_parts, "shard", scatter_dimension=0, tiled=True)
    hot_grad = lax.psum(item_grad, "grp")
    devices = cold_requests.shape[1]
    slot_count = cold_requests.shape[2]
    requests = cold_requests.reshape(devices, slot_count)
    live_slots = lax.iota(jnp.int32, slot_count)[None, :] < cold_counts.reshape(devices, 1)
    asked_rows = lax.all_to_all(requests, ("grp", "shard"), split_axis=0, concat_axis=0, tiled=True)
    found = onehot_gather(cold_half, asked_rows.reshape(-1))
    fetched = lax.all_to_all(
        found.reshape(devices, slot_count, feature_count),
        ("grp", "shard"),
        split_axis=0,
        concat_axis=0,
        tiled=True,
    )
    flat_rows = fetched.reshape(devices * slot_count, feature_count)
    scores = jnp.einsum("uk,rk->ur", user_half, flat_rows, preferred_element_type=jnp.float32)
    weights = (jax.nn.sigmoid(scores) * live_slots.reshape(1, -1).astype(jnp.float32)).astype(
        jnp.bfloat16
    )
    user_cold = jnp.dot(weights, flat_rows, preferred_element_type=jnp.float32)
    row_terms = jnp.einsum(
        "ur,uk->rk", weights, user_half, preferred_element_type=jnp.float32
    ).astype(jnp.bfloat16)
    row_terms = row_terms.reshape(devices, slot_count, feature_count)
    returned = lax.all_to_all(row_terms, ("grp", "shard"), split_axis=0, concat_axis=0, tiled=True)
    cold_grad = onehot_scatter_add(
        asked_rows.reshape(-1),
        returned.reshape(devices * slot_count, feature_count),
        cold_table.shape[0],
    )
    user_grad = user_hot + user_cold
    new_users, new_user_accum = adagrad(users, user_accum, user_grad)
    new_hot, new_hot_accum = adagrad(hot_table, hot_accum, hot_grad)
    new_cold, new_cold_accum = adagrad(cold_table, cold_accum, cold_grad)
    return (new_users, new_user_accum, new_hot, new_hot_accum, new_cold, new_cold_accum)


def solution(mesh):
    return jax.shard_map(
        body,
        mesh=mesh,
        in_specs=(
            P(("grp", "shard"), None),
            P(("grp", "shard"), None),
            P(("grp", "shard"), None),
            P("shard", None),
            P("shard", None),
            P(("grp", "shard"), None),
            P(("grp", "shard"), None),
            P(("grp", "shard"), None, None),
            P(("grp", "shard"), None),
        ),
        out_specs=(
            P(("grp", "shard"), None),
            P(("grp", "shard"), None),
            P("shard", None),
            P("shard", None),
            P(("grp", "shard"), None),
            P(("grp", "shard"), None),
        ),
        check_vma=False,
    )
```

```python
import functools

import jax
import jax.numpy as jnp
from jax import lax
from jax.experimental import pallas as pl
from jax.experimental.pallas import tpu as pltpu
from jax.sharding import Mesh, PartitionSpec as P

POSITIVE_WEIGHT = 32.0
LEARN_RATE = 0.5
LANES = 128
SUB = 8


def _nt(a, b):
    return lax.dot_general(a, b, (((1,), (1,)), ((), ())), preferred_element_type=jnp.float32)


def _tn(a, b):
    return lax.dot_general(a, b, (((0,), (0,)), ((), ())), preferred_element_type=jnp.float32)


def _hot_kernel(u_ref, h_ref, ph_ref, pl_ref, up_ref, ip_ref, m_ref, *, sub_users):
    i = pl.program_id(0)
    items = h_ref.shape[0]
    nh = items // LANES
    subtiles = ph_ref.shape[0]
    width = ph_ref.shape[1]
    per = width // sub_users
    r = lax.broadcasted_iota(jnp.int32, (nh * sub_users, width), 0)
    c = lax.broadcasted_iota(jnp.int32, (nh * sub_users, width), 1)
    diag = (r % sub_users) == (c // per)
    hrow = r // sub_users
    lrow = lax.broadcasted_iota(jnp.int32, (LANES, width), 0)

    def sub(s, carry):
        lhs = jnp.where(diag & (ph_ref[pl.ds(s, 1), :] == hrow), 1.0, 0.0).astype(jnp.bfloat16)
        rhs = jnp.where(pl_ref[pl.ds(s, 1), :] == lrow, 1.0, 0.0).astype(jnp.bfloat16)
        out = _nt(lhs, rhs)
        base = pl.multiple_of(s * sub_users, sub_users)
        for h in range(nh):
            m_ref[pl.ds(base, sub_users), pl.ds(h * LANES, LANES)] = out[
                h * sub_users:(h + 1) * sub_users, :
            ]
        return carry

    lax.fori_loop(0, subtiles, sub, 0, unroll=subtiles)
    u = u_ref[...]
    hj = h_ref[...]
    scores = _nt(u, hj)
    m = m_ref[...]
    w = ((1.0 + POSITIVE_WEIGHT * m) * jax.nn.sigmoid(scores) - POSITIVE_WEIGHT * m).astype(
        jnp.bfloat16
    )
    up_ref[...] = jnp.dot(w, hj, preferred_element_type=jnp.float32)

    @pl.when(i == 0)
    def _():
        ip_ref[...] = jnp.zeros_like(ip_ref)

    ip_ref[...] += _tn(w, u)


def hot_terms(user_half, positives, hot_rows, tile=512, sub_users=8):
    users, k = user_half.shape
    items = hot_rows.shape[0]
    pos_count = positives.shape[1]
    subtiles = users // sub_users
    width = sub_users * pos_count
    pos_hi = (positives // LANES).reshape(subtiles, width)
    pos_lo = (positives % LANES).reshape(subtiles, width)
    per_tile = tile // sub_users
    return pl.pallas_call(
        functools.partial(_hot_kernel, sub_users=sub_users),
        grid=(users // tile,),
        in_specs=[
            pl.BlockSpec((tile, k), lambda i: (i, 0)),
            pl.BlockSpec((items, k), lambda i: (0, 0)),
            pl.BlockSpec((per_tile, width), lambda i: (i, 0)),
            pl.BlockSpec((per_tile, width), lambda i: (i, 0)),
        ],
        out_specs=[
            pl.BlockSpec((tile, k), lambda i: (i, 0)),
            pl.BlockSpec((items, k), lambda i: (0, 0)),
        ],
        out_shape=[
            jax.ShapeDtypeStruct((users, k), jnp.float32),
            jax.ShapeDtypeStruct((items, k), jnp.float32),
        ],
        scratch_shapes=[pltpu.VMEM((tile, items), jnp.float32)],
        compiler_params=pltpu.CompilerParams(dimension_semantics=("arbitrary",)),
    )(user_half, hot_rows, pos_hi, pos_lo)


def _gather_kernel(idx_ref, table_ref, out_ref):
    rows = table_ref.shape[0]
    onehot = (idx_ref[...] == lax.broadcasted_iota(jnp.int32, (1, rows), 1)).astype(jnp.bfloat16)
    out_ref[...] = jnp.dot(onehot, table_ref[...], preferred_element_type=jnp.float32).astype(
        out_ref.dtype
    )


def onehot_gather(table, idx, chunk=1024):
    rows, k = table.shape
    n = idx.shape[0]
    return pl.pallas_call(
        _gather_kernel,
        grid=(n // chunk,),
        in_specs=[
            pl.BlockSpec((chunk, 1), lambda i: (i, 0)),
            pl.BlockSpec((rows, k), lambda i: (0, 0)),
        ],
        out_specs=pl.BlockSpec((chunk, k), lambda i: (i, 0)),
        out_shape=jax.ShapeDtypeStruct((n, k), table.dtype),
    )(idx.reshape(n, 1), table)


def _scatter_kernel(idx_ref, val_ref, out_ref):
    i = pl.program_id(0)
    rows = out_ref.shape[0]
    chunk = idx_ref.shape[1]
    onehot = (idx_ref[...] == lax.broadcasted_iota(jnp.int32, (rows, chunk), 0)).astype(
        jnp.bfloat16
    )

    @pl.when(i == 0)
    def _():
        out_ref[...] = jnp.zeros_like(out_ref)

    out_ref[...] += jnp.dot(onehot, val_ref[...], preferred_element_type=jnp.float32)


def onehot_scatter_add(idx, values, rows, chunk=1024):
    n, k = values.shape
    return pl.pallas_call(
        _scatter_kernel,
        grid=(n // chunk,),
        in_specs=[
            pl.BlockSpec((1, chunk), lambda i: (0, i)),
            pl.BlockSpec((chunk, k), lambda i: (i, 0)),
        ],
        out_specs=pl.BlockSpec((rows, k), lambda i: (0, 0)),
        out_shape=jax.ShapeDtypeStruct((rows, k), jnp.float32),
        compiler_params=pltpu.CompilerParams(dimension_semantics=("arbitrary",)),
    )(idx.reshape(1, n), values)


def adagrad(current, history, gradient):
    updated = history + gradient * gradient
    return (current - LEARN_RATE * gradient / jnp.sqrt(updated), updated)


def body(
    users,
    user_accum,
    positives,
    hot_table,
    hot_accum,
    cold_table,
    cold_accum,
    cold_requests,
    cold_counts,
):
    user_half = users.astype(jnp.bfloat16)
    hot_half = hot_table.astype(jnp.bfloat16)
    cold_half = cold_table.astype(jnp.bfloat16)
    feature_count = users.shape[1]
    item_sub = hot_table.shape[0]
    sb_count = lax.axis_size("sb")
    users_part = lax.all_gather(user_half, "sb", axis=0, tiled=True)
    pos_part = lax.all_gather(positives, "sb", axis=0, tiled=True)
    hot_part = lax.all_gather(hot_half, "sa", axis=0, tiled=True)
    owner = pos_part // item_sub
    local = (owner // sb_count) * item_sub + pos_part % item_sub
    local = jnp.where(owner % sb_count == lax.axis_index("sb"), local, hot_part.shape[0])
    user_hot_part, item_part = hot_terms(users_part, local, hot_part)
    user_hot = lax.psum_scatter(user_hot_part, "sb", scatter_dimension=0, tiled=True)
    item_grad = lax.psum_scatter(item_part, "sa", scatter_dimension=0, tiled=True)
    hot_grad = lax.psum(item_grad, "grp")
    devices = cold_requests.shape[1]
    slot_count = cold_requests.shape[2]
    requests = cold_requests.reshape(devices, slot_count)
    live_slots = lax.iota(jnp.int32, slot_count)[None, :] < cold_counts.reshape(devices, 1)
    asked_rows = lax.all_to_all(requests, ("grp", "sa", "sb"), split_axis=0, concat_axis=0, tiled=True)
    found = onehot_gather(cold_half, asked_rows.reshape(-1))
    fetched = lax.all_to_all(
        found.reshape(devices, slot_count, feature_count),
        ("grp", "sa", "sb"),
        split_axis=0,
        concat_axis=0,
        tiled=True,
    )
    flat_rows = fetched.reshape(devices * slot_count, feature_count)
    scores = jnp.einsum("uk,rk->ur", user_half, flat_rows, preferred_element_type=jnp.float32)
    weights = (jax.nn.sigmoid(scores) * live_slots.reshape(1, -1).astype(jnp.float32)).astype(
        jnp.bfloat16
    )
    user_cold = jnp.dot(weights, flat_rows, preferred_element_type=jnp.float32)
    row_terms = jnp.einsum(
        "ur,uk->rk", weights, user_half, preferred_element_type=jnp.float32
    ).astype(jnp.bfloat16)
    row_terms = row_terms.reshape(devices, slot_count, feature_count)
    returned = lax.all_to_all(row_terms, ("grp", "sa", "sb"), split_axis=0, concat_axis=0, tiled=True)
    cold_grad = onehot_scatter_add(
        asked_rows.reshape(-1),
        returned.reshape(devices * slot_count, feature_count),
        cold_table.shape[0],
    )
    user_grad = user_hot + user_cold
    new_users, new_user_accum = adagrad(users, user_accum, user_grad)
    new_hot, new_hot_accum = adagrad(hot_table, hot_accum, hot_grad)
    new_cold, new_cold_accum = adagrad(cold_table, cold_accum, cold_grad)
    return (new_users, new_user_accum, new_hot, new_hot_accum, new_cold, new_cold_accum)


def _split_mesh(mesh):
    shard = mesh.shape["shard"]
    sa = 4 if shard % 4 == 0 else 1
    return Mesh(mesh.devices.reshape(mesh.shape["grp"], sa, shard // sa), ("grp", "sa", "sb"))


def solution(mesh):
    return jax.shard_map(
        body,
        mesh=_split_mesh(mesh),
        in_specs=(
            P(("grp", "sa", "sb"), None),
            P(("grp", "sa", "sb"), None),
            P(("grp", "sa", "sb"), None),
            P(("sa", "sb"), None),
            P(("sa", "sb"), None),
            P(("grp", "sa", "sb"), None),
            P(("grp", "sa", "sb"), None),
            P(("grp", "sa", "sb"), None, None),
            P(("grp", "sa", "sb"), None),
        ),
        out_specs=(
            P(("grp", "sa", "sb"), None),
            P(("grp", "sa", "sb"), None),
            P(("sa", "sb"), None),
            P(("sa", "sb"), None),
            P(("grp", "sa", "sb"), None),
            P(("grp", "sa", "sb"), None),
        ),
        check_vma=False,
    )
```

```python
import functools

import jax
import jax.numpy as jnp
from jax import lax
from jax.experimental import pallas as pl
from jax.experimental.pallas import tpu as pltpu
from jax.sharding import Mesh, PartitionSpec as P

POSITIVE_WEIGHT = 32.0
LEARN_RATE = 0.5
LANES = 128
SUB = 8


def _nt(a, b):
    return lax.dot_general(a, b, (((1,), (1,)), ((), ())), preferred_element_type=jnp.float32)


def _tn(a, b):
    return lax.dot_general(a, b, (((0,), (0,)), ((), ())), preferred_element_type=jnp.float32)


def _hot_kernel(u_ref, h_ref, ph_ref, pl_ref, up_ref, ip_ref, m_ref, *, sub_users):
    i = pl.program_id(0)
    items = h_ref.shape[0]
    nh = items // LANES
    subtiles = ph_ref.shape[0]
    width = ph_ref.shape[1]
    per = width // sub_users
    r = lax.broadcasted_iota(jnp.int32, (nh * sub_users, width), 0)
    c = lax.broadcasted_iota(jnp.int32, (nh * sub_users, width), 1)
    diag = (r % sub_users) == (c // per)
    hrow = r // sub_users
    lrow = lax.broadcasted_iota(jnp.int32, (LANES, width), 0)

    def sub(s, carry):
        lhs = jnp.where(diag & (ph_ref[pl.ds(s, 1), :] == hrow), 1.0, 0.0).astype(jnp.bfloat16)
        rhs = jnp.where(pl_ref[pl.ds(s, 1), :] == lrow, 1.0, 0.0).astype(jnp.bfloat16)
        out = _nt(lhs, rhs)
        base = pl.multiple_of(s * sub_users, sub_users)
        for h in range(nh):
            m_ref[pl.ds(base, sub_users), pl.ds(h * LANES, LANES)] = out[
                h * sub_users:(h + 1) * sub_users, :
            ]
        return carry

    lax.fori_loop(0, subtiles, sub, 0, unroll=subtiles)
    u = u_ref[...]
    hj = h_ref[...]
    scores = _nt(u, hj)
    m = m_ref[...]
    w = ((1.0 + POSITIVE_WEIGHT * m) * jax.nn.sigmoid(scores) - POSITIVE_WEIGHT * m).astype(
        jnp.bfloat16
    )
    up_ref[...] = jnp.dot(w, hj, preferred_element_type=jnp.float32)

    @pl.when(i == 0)
    def _():
        ip_ref[...] = jnp.zeros_like(ip_ref)

    ip_ref[...] += _tn(w, u)


def hot_terms(user_half, positives, hot_rows, tile=512, sub_users=8):
    users, k = user_half.shape
    items = hot_rows.shape[0]
    pos_count = positives.shape[1]
    subtiles = users // sub_users
    width = sub_users * pos_count
    pos_hi = (positives // LANES).reshape(subtiles, width)
    pos_lo = (positives % LANES).reshape(subtiles, width)
    per_tile = tile // sub_users
    return pl.pallas_call(
        functools.partial(_hot_kernel, sub_users=sub_users),
        grid=(users // tile,),
        in_specs=[
            pl.BlockSpec((tile, k), lambda i: (i, 0)),
            pl.BlockSpec((items, k), lambda i: (0, 0)),
            pl.BlockSpec((per_tile, width), lambda i: (i, 0)),
            pl.BlockSpec((per_tile, width), lambda i: (i, 0)),
        ],
        out_specs=[
            pl.BlockSpec((tile, k), lambda i: (i, 0)),
            pl.BlockSpec((items, k), lambda i: (0, 0)),
        ],
        out_shape=[
            jax.ShapeDtypeStruct((users, k), jnp.float32),
            jax.ShapeDtypeStruct((items, k), jnp.float32),
        ],
        scratch_shapes=[pltpu.VMEM((tile, items), jnp.float32)],
        compiler_params=pltpu.CompilerParams(dimension_semantics=("arbitrary",)),
    )(user_half, hot_rows, pos_hi, pos_lo)


def _gather_kernel(idx_ref, table_ref, out_ref):
    rows = table_ref.shape[0]
    onehot = (idx_ref[...] == lax.broadcasted_iota(jnp.int32, (1, rows), 1)).astype(jnp.bfloat16)
    out_ref[...] = jnp.dot(onehot, table_ref[...], preferred_element_type=jnp.float32).astype(
        out_ref.dtype
    )


def onehot_gather(table, idx, chunk=1024):
    rows, k = table.shape
    n = idx.shape[0]
    return pl.pallas_call(
        _gather_kernel,
        grid=(n // chunk,),
        in_specs=[
            pl.BlockSpec((chunk, 1), lambda i: (i, 0)),
            pl.BlockSpec((rows, k), lambda i: (0, 0)),
        ],
        out_specs=pl.BlockSpec((chunk, k), lambda i: (i, 0)),
        out_shape=jax.ShapeDtypeStruct((n, k), table.dtype),
    )(idx.reshape(n, 1), table)


def _scatter_kernel(idx_ref, val_ref, out_ref):
    i = pl.program_id(0)
    rows = out_ref.shape[0]
    chunk = idx_ref.shape[1]
    onehot = (idx_ref[...] == lax.broadcasted_iota(jnp.int32, (rows, chunk), 0)).astype(
        jnp.bfloat16
    )

    @pl.when(i == 0)
    def _():
        out_ref[...] = jnp.zeros_like(out_ref)

    out_ref[...] += jnp.dot(onehot, val_ref[...], preferred_element_type=jnp.float32)


def onehot_scatter_add(idx, values, rows, chunk=1024):
    n, k = values.shape
    return pl.pallas_call(
        _scatter_kernel,
        grid=(n // chunk,),
        in_specs=[
            pl.BlockSpec((1, chunk), lambda i: (0, i)),
            pl.BlockSpec((chunk, k), lambda i: (i, 0)),
        ],
        out_specs=pl.BlockSpec((rows, k), lambda i: (0, 0)),
        out_shape=jax.ShapeDtypeStruct((rows, k), jnp.float32),
        compiler_params=pltpu.CompilerParams(dimension_semantics=("arbitrary",)),
    )(idx.reshape(1, n), values)


def adagrad(current, history, gradient):
    updated = history + gradient * gradient
    return (current - LEARN_RATE * gradient / jnp.sqrt(updated), updated)


def body(
    users,
    user_accum,
    positives,
    hot_table,
    hot_accum,
    cold_table,
    cold_accum,
    cold_requests,
    cold_counts,
):
    user_half = users.astype(jnp.bfloat16)
    hot_half = hot_table.astype(jnp.bfloat16)
    cold_half = cold_table.astype(jnp.bfloat16)
    feature_count = users.shape[1]
    item_sub = hot_table.shape[0]
    sb_count = lax.axis_size("sb")
    pos_count = positives.shape[1]
    devices = cold_requests.shape[1]
    slot_count = cold_requests.shape[2]
    requests = cold_requests.reshape(devices, slot_count)
    live_slots = lax.iota(jnp.int32, slot_count)[None, :] < cold_counts.reshape(devices, 1)
    asked_rows = lax.all_to_all(requests, ("grp", "sa", "sb"), split_axis=0, concat_axis=0, tiled=True)
    found = onehot_gather(cold_half, asked_rows.reshape(-1))
    packed = jnp.concatenate(
        [user_half, (positives // LANES).astype(jnp.bfloat16), (positives % LANES).astype(jnp.bfloat16)],
        axis=1,
    )
    packed_part = lax.all_gather(packed, "sb", axis=0, tiled=True)
    hot_part = lax.all_gather(hot_half, "sa", axis=0, tiled=True)
    found, packed_part, hot_part = lax.optimization_barrier((found, packed_part, hot_part))
    fetched = lax.all_to_all(
        found.reshape(devices, slot_count, feature_count),
        ("grp", "sa", "sb"),
        split_axis=0,
        concat_axis=0,
        tiled=True,
    )
    users_part = packed_part[:, :feature_count]
    pos_hi = packed_part[:, feature_count:feature_count + pos_count].astype(jnp.int32)
    pos_lo = packed_part[:, feature_count + pos_count:].astype(jnp.int32)
    hi_per_item = item_sub // LANES
    owner = pos_hi // hi_per_item
    local_hi = (owner // sb_count) * hi_per_item + pos_hi % hi_per_item
    local = jnp.where(owner % sb_count == lax.axis_index("sb"), local_hi * LANES + pos_lo, hot_part.shape[0])
    user_hot_part, item_part = hot_terms(users_part, local, hot_part)
    fetched, user_hot_part, item_part = lax.optimization_barrier((fetched, user_hot_part, item_part))
    user_hot = lax.psum_scatter(user_hot_part, "sb", scatter_dimension=0, tiled=True)
    item_grad = lax.psum_scatter(item_part, "sa", scatter_dimension=0, tiled=True)
    hot_grad = lax.psum(item_grad, "grp")
    flat_rows = fetched.reshape(devices * slot_count, feature_count)
    scores = jnp.einsum("uk,rk->ur", user_half, flat_rows, preferred_element_type=jnp.float32)
    weights = (jax.nn.sigmoid(scores) * live_slots.reshape(1, -1).astype(jnp.float32)).astype(
        jnp.bfloat16
    )
    user_cold = jnp.dot(weights, flat_rows, preferred_element_type=jnp.float32)
    row_terms = jnp.einsum(
        "ur,uk->rk", weights, user_half, preferred_element_type=jnp.float32
    ).astype(jnp.bfloat16)
    row_terms = row_terms.reshape(devices, slot_count, feature_count)
    returned = lax.all_to_all(row_terms, ("grp", "sa", "sb"), split_axis=0, concat_axis=0, tiled=True)
    cold_grad = onehot_scatter_add(
        asked_rows.reshape(-1),
        returned.reshape(devices * slot_count, feature_count),
        cold_table.shape[0],
    )
    user_grad = user_hot + user_cold
    new_users, new_user_accum = adagrad(users, user_accum, user_grad)
    new_hot, new_hot_accum = adagrad(hot_table, hot_accum, hot_grad)
    new_cold, new_cold_accum = adagrad(cold_table, cold_accum, cold_grad)
    return (new_users, new_user_accum, new_hot, new_hot_accum, new_cold, new_cold_accum)


def _split_mesh(mesh):
    shard = mesh.shape["shard"]
    sa = 4 if shard % 4 == 0 else 1
    return Mesh(mesh.devices.reshape(mesh.shape["grp"], sa, shard // sa), ("grp", "sa", "sb"))


def solution(mesh):
    return jax.shard_map(
        body,
        mesh=_split_mesh(mesh),
        in_specs=(
            P(("grp", "sa", "sb"), None),
            P(("grp", "sa", "sb"), None),
            P(("grp", "sa", "sb"), None),
            P(("sa", "sb"), None),
            P(("sa", "sb"), None),
            P(("grp", "sa", "sb"), None),
            P(("grp", "sa", "sb"), None),
            P(("grp", "sa", "sb"), None, None),
            P(("grp", "sa", "sb"), None),
        ),
        out_specs=(
            P(("grp", "sa", "sb"), None),
            P(("grp", "sa", "sb"), None),
            P(("sa", "sb"), None),
            P(("sa", "sb"), None),
            P(("grp", "sa", "sb"), None),
            P(("grp", "sa", "sb"), None),
        ),
        check_vma=False,
    )
```

```python
import functools

import jax
import jax.numpy as jnp
from jax import lax
from jax.experimental import pallas as pl
from jax.experimental.pallas import tpu as pltpu
from jax.sharding import Mesh, PartitionSpec as P

POSITIVE_WEIGHT = 32.0
LEARN_RATE = 0.5
LANES = 128
SUB = 8


def _nt(a, b):
    return lax.dot_general(a, b, (((1,), (1,)), ((), ())), preferred_element_type=jnp.float32)


def _tn(a, b):
    return lax.dot_general(a, b, (((0,), (0,)), ((), ())), preferred_element_type=jnp.float32)


def _hot_kernel(u_ref, h_ref, ph_ref, pl_ref, dep_ref, *rest, sub_users, chained):
    del dep_ref
    if chained:
        _, ipin_ref, up_ref, ip_ref, m_ref = rest
    else:
        up_ref, ip_ref, m_ref = rest
    i = pl.program_id(0)
    items = h_ref.shape[0]
    nh = items // LANES
    subtiles = ph_ref.shape[0]
    width = ph_ref.shape[1]
    per = width // sub_users
    r = lax.broadcasted_iota(jnp.int32, (nh * sub_users, width), 0)
    c = lax.broadcasted_iota(jnp.int32, (nh * sub_users, width), 1)
    diag = (r % sub_users) == (c // per)
    hrow = r // sub_users
    lrow = lax.broadcasted_iota(jnp.int32, (LANES, width), 0)

    def sub(s, carry):
        lhs = jnp.where(diag & (ph_ref[pl.ds(s, 1), :] == hrow), 1.0, 0.0).astype(jnp.bfloat16)
        rhs = jnp.where(pl_ref[pl.ds(s, 1), :] == lrow, 1.0, 0.0).astype(jnp.bfloat16)
        out = _nt(lhs, rhs)
        base = pl.multiple_of(s * sub_users, sub_users)
        for h in range(nh):
            m_ref[pl.ds(base, sub_users), pl.ds(h * LANES, LANES)] = out[
                h * sub_users:(h + 1) * sub_users, :
            ]
        return carry

    lax.fori_loop(0, subtiles, sub, 0, unroll=subtiles)
    u = u_ref[...]
    hj = h_ref[...]
    scores = _nt(u, hj)
    m = m_ref[...]
    w = ((1.0 + POSITIVE_WEIGHT * m) * jax.nn.sigmoid(scores) - POSITIVE_WEIGHT * m).astype(
        jnp.bfloat16
    )
    up_ref[...] = jnp.dot(w, hj, preferred_element_type=jnp.float32)

    @pl.when(i == 0)
    def _():
        if chained:
            ip_ref[...] = ipin_ref[...]
        else:
            ip_ref[...] = jnp.zeros_like(ip_ref)

    ip_ref[...] += _tn(w, u)


def hot_prepare(positives, sub_users=8):
    users, pos_count = positives.shape
    subtiles = users // sub_users
    width = sub_users * pos_count
    return (
        (positives // LANES).reshape(subtiles, width),
        (positives % LANES).reshape(subtiles, width),
    )


def hot_terms(user_half, pos_hi, pos_lo, hot_rows, first, count, dep, prev=None, tile=512, sub_users=8):
    users, k = user_half.shape
    items = hot_rows.shape[0]
    width = pos_hi.shape[1]
    per_tile = tile // sub_users
    in_specs = [
        pl.BlockSpec((tile, k), lambda i: (first + i, 0)),
        pl.BlockSpec((items, k), lambda i: (0, 0)),
        pl.BlockSpec((per_tile, width), lambda i: (first + i, 0)),
        pl.BlockSpec((per_tile, width), lambda i: (first + i, 0)),
        pl.BlockSpec(memory_space=pl.ANY),
    ]
    args = [user_half, hot_rows, pos_hi, pos_lo, dep]
    aliases = {}
    if prev is not None:
        in_specs += [pl.BlockSpec(memory_space=pl.ANY), pl.BlockSpec((items, k), lambda i: (0, 0))]
        args += list(prev)
        aliases = {5: 0, 6: 1}
    return pl.pallas_call(
        functools.partial(_hot_kernel, sub_users=sub_users, chained=prev is not None),
        grid=(count,),
        in_specs=in_specs,
        out_specs=[
            pl.BlockSpec((tile, k), lambda i: (first + i, 0)),
            pl.BlockSpec((items, k), lambda i: (0, 0)),
        ],
        out_shape=[
            jax.ShapeDtypeStruct((users, k), jnp.float32),
            jax.ShapeDtypeStruct((items, k), jnp.float32),
        ],
        scratch_shapes=[pltpu.VMEM((tile, items), jnp.float32)],
        input_output_aliases=aliases,
        compiler_params=pltpu.CompilerParams(dimension_semantics=("arbitrary",)),
    )(*args)


def _gather_kernel(idx_ref, table_ref, out_ref):
    rows = table_ref.shape[0]
    chunk = idx_ref.shape[1]
    onehot = (idx_ref[...] == lax.broadcasted_iota(jnp.int32, (rows, chunk), 0)).astype(
        jnp.bfloat16
    )
    out_ref[...] = _tn(onehot, table_ref[...]).astype(out_ref.dtype)


def onehot_gather(table, idx, chunk=1024):
    rows, k = table.shape
    n = idx.shape[0]
    return pl.pallas_call(
        _gather_kernel,
        grid=(n // chunk,),
        in_specs=[
            pl.BlockSpec((1, chunk), lambda i: (0, i)),
            pl.BlockSpec((rows, k), lambda i: (0, 0)),
        ],
        out_specs=pl.BlockSpec((chunk, k), lambda i: (i, 0)),
        out_shape=jax.ShapeDtypeStruct((n, k), table.dtype),
    )(idx.reshape(1, n), table)


def _scatter_kernel(idx_ref, val_ref, out_ref):
    i = pl.program_id(0)
    rows = out_ref.shape[0]
    chunk = idx_ref.shape[1]
    onehot = (idx_ref[...] == lax.broadcasted_iota(jnp.int32, (rows, chunk), 0)).astype(
        jnp.bfloat16
    )

    @pl.when(i == 0)
    def _():
        out_ref[...] = jnp.zeros_like(out_ref)

    out_ref[...] += jnp.dot(onehot, val_ref[...], preferred_element_type=jnp.float32)


def onehot_scatter_add(idx, values, rows, chunk=1024):
    n, k = values.shape
    return pl.pallas_call(
        _scatter_kernel,
        grid=(n // chunk,),
        in_specs=[
            pl.BlockSpec((1, chunk), lambda i: (0, i)),
            pl.BlockSpec((chunk, k), lambda i: (i, 0)),
        ],
        out_specs=pl.BlockSpec((rows, k), lambda i: (0, 0)),
        out_shape=jax.ShapeDtypeStruct((rows, k), jnp.float32),
        compiler_params=pltpu.CompilerParams(dimension_semantics=("arbitrary",)),
    )(idx.reshape(1, n), values)


def adagrad(current, history, gradient):
    updated = history + gradient * gradient
    return (current - LEARN_RATE * gradient / jnp.sqrt(updated), updated)


def body(
    users,
    user_accum,
    positives,
    hot_table,
    hot_accum,
    cold_table,
    cold_accum,
    cold_requests,
    cold_counts,
):
    user_half = users.astype(jnp.bfloat16)
    hot_half = hot_table.astype(jnp.bfloat16)
    cold_half = cold_table.astype(jnp.bfloat16)
    feature_count = users.shape[1]
    item_sub = hot_table.shape[0]
    sb_count = lax.axis_size("sb")
    pos_count = positives.shape[1]
    devices = cold_requests.shape[1]
    slot_count = cold_requests.shape[2]
    requests = cold_requests.reshape(devices, slot_count)
    live_slots = lax.iota(jnp.int32, slot_count)[None, :] < cold_counts.reshape(devices, 1)
    asked_rows = lax.all_to_all(requests, ("grp", "sa", "sb"), split_axis=0, concat_axis=0, tiled=True)
    found = onehot_gather(cold_half, asked_rows.reshape(-1))
    packed = jnp.concatenate(
        [user_half, (positives // LANES).astype(jnp.bfloat16), (positives % LANES).astype(jnp.bfloat16)],
        axis=1,
    )
    packed_part = lax.all_gather(packed, "sb", axis=0, tiled=True)
    hot_part = lax.all_gather(hot_half, "sa", axis=0, tiled=True)
    fetched = lax.all_to_all(
        found.reshape(devices, slot_count, feature_count),
        ("grp", "sa", "sb"),
        split_axis=0,
        concat_axis=0,
        tiled=True,
    )
    users_part = packed_part[:, :feature_count]
    pos_hi = packed_part[:, feature_count:feature_count + pos_count].astype(jnp.int32)
    pos_lo = packed_part[:, feature_count + pos_count:].astype(jnp.int32)
    hi_per_item = item_sub // LANES
    owner = pos_hi // hi_per_item
    local_hi = (owner // sb_count) * hi_per_item + pos_hi % hi_per_item
    local = jnp.where(owner % sb_count == lax.axis_index("sb"), local_hi * LANES + pos_lo, hot_part.shape[0])
    pos_hi_t, pos_lo_t = hot_prepare(local)
    tiles = users_part.shape[0] // 512
    half = tiles // 2
    part_a = hot_terms(users_part, pos_hi_t, pos_lo_t, hot_part, 0, half, found)
    fetched, part_a = lax.optimization_barrier((fetched, part_a))
    flat_rows = fetched.reshape(devices * slot_count, feature_count)
    scores = jnp.einsum("uk,rk->ur", user_half, flat_rows, preferred_element_type=jnp.float32)
    weights = (jax.nn.sigmoid(scores) * live_slots.reshape(1, -1).astype(jnp.float32)).astype(
        jnp.bfloat16
    )
    user_cold = jnp.dot(weights, flat_rows, preferred_element_type=jnp.float32)
    row_terms = jnp.einsum(
        "ur,uk->rk", weights, user_half, preferred_element_type=jnp.float32
    ).astype(jnp.bfloat16)
    row_terms = row_terms.reshape(devices, slot_count, feature_count)
    returned = lax.all_to_all(row_terms, ("grp", "sa", "sb"), split_axis=0, concat_axis=0, tiled=True)
    user_hot_part, item_part = hot_terms(
        users_part, pos_hi_t, pos_lo_t, hot_part, half, tiles - half, row_terms, prev=part_a
    )
    returned, user_hot_part, item_part = lax.optimization_barrier((returned, user_hot_part, item_part))
    user_hot = lax.psum_scatter(user_hot_part, "sb", scatter_dimension=0, tiled=True)
    item_grad = lax.psum_scatter(item_part, "sa", scatter_dimension=0, tiled=True)
    hot_grad = lax.psum(item_grad, "grp")
    cold_grad = onehot_scatter_add(
        asked_rows.reshape(-1),
        returned.reshape(devices * slot_count, feature_count),
        cold_table.shape[0],
    )
    user_grad = user_hot + user_cold
    new_users, new_user_accum = adagrad(users, user_accum, user_grad)
    new_hot, new_hot_accum = adagrad(hot_table, hot_accum, hot_grad)
    new_cold, new_cold_accum = adagrad(cold_table, cold_accum, cold_grad)
    return (new_users, new_user_accum, new_hot, new_hot_accum, new_cold, new_cold_accum)


def _split_mesh(mesh):
    shard = mesh.shape["shard"]
    sa = 4 if shard % 4 == 0 else 1
    return Mesh(mesh.devices.reshape(mesh.shape["grp"], sa, shard // sa), ("grp", "sa", "sb"))


def solution(mesh):
    return jax.shard_map(
        body,
        mesh=_split_mesh(mesh),
        in_specs=(
            P(("grp", "sa", "sb"), None),
            P(("grp", "sa", "sb"), None),
            P(("grp", "sa", "sb"), None),
            P(("sa", "sb"), None),
            P(("sa", "sb"), None),
            P(("grp", "sa", "sb"), None),
            P(("grp", "sa", "sb"), None),
            P(("grp", "sa", "sb"), None, None),
            P(("grp", "sa", "sb"), None),
        ),
        out_specs=(
            P(("grp", "sa", "sb"), None),
            P(("grp", "sa", "sb"), None),
            P(("sa", "sb"), None),
            P(("sa", "sb"), None),
            P(("grp", "sa", "sb"), None),
            P(("grp", "sa", "sb"), None),
        ),
        check_vma=False,
    )
```

```python
import functools

import jax
import jax.numpy as jnp
from jax import lax
from jax.experimental import pallas as pl
from jax.experimental.pallas import tpu as pltpu
from jax.sharding import Mesh, PartitionSpec as P

POSITIVE_WEIGHT = 32.0
LEARN_RATE = 0.5
LANES = 128
SUB = 8


def _nt(a, b):
    return lax.dot_general(a, b, (((1,), (1,)), ((), ())), preferred_element_type=jnp.float32)


def _tn(a, b):
    return lax.dot_general(a, b, (((0,), (0,)), ((), ())), preferred_element_type=jnp.float32)


def _hot_kernel(u_ref, h_ref, ph_ref, pl_ref, dep_ref, *rest, sub_users, chained):
    del dep_ref
    if chained:
        _, ipin_ref, up_ref, ip_ref, m_ref = rest
    else:
        up_ref, ip_ref, m_ref = rest
    i = pl.program_id(0)
    items = h_ref.shape[0]
    nh = items // LANES
    subtiles = ph_ref.shape[0]
    width = ph_ref.shape[1]
    per = width // sub_users
    r = lax.broadcasted_iota(jnp.int32, (nh * sub_users, width), 0)
    c = lax.broadcasted_iota(jnp.int32, (nh * sub_users, width), 1)
    diag = (r % sub_users) == (c // per)
    hrow = r // sub_users
    lrow = lax.broadcasted_iota(jnp.int32, (LANES, width), 0)

    def sub(s, carry):
        lhs = jnp.where(diag & (ph_ref[pl.ds(s, 1), :] == hrow), 1.0, 0.0).astype(jnp.bfloat16)
        rhs = jnp.where(pl_ref[pl.ds(s, 1), :] == lrow, 1.0, 0.0).astype(jnp.bfloat16)
        out = _nt(lhs, rhs)
        base = pl.multiple_of(s * sub_users, sub_users)
        for h in range(nh):
            m_ref[pl.ds(base, sub_users), pl.ds(h * LANES, LANES)] = out[
                h * sub_users:(h + 1) * sub_users, :
            ]
        return carry

    lax.fori_loop(0, subtiles, sub, 0, unroll=subtiles)
    u = u_ref[...]
    hj = h_ref[...]
    scores = _nt(u, hj)
    m = m_ref[...]
    w = ((1.0 + POSITIVE_WEIGHT * m) * jax.nn.sigmoid(scores) - POSITIVE_WEIGHT * m).astype(
        jnp.bfloat16
    )
    up_ref[...] = jnp.dot(w, hj, preferred_element_type=jnp.float32)

    @pl.when(i == 0)
    def _():
        if chained:
            ip_ref[...] = ipin_ref[...]
        else:
            ip_ref[...] = jnp.zeros_like(ip_ref)

    ip_ref[...] += _tn(w, u)


def hot_prepare(positives, sub_users=8):
    users, pos_count = positives.shape
    subtiles = users // sub_users
    width = sub_users * pos_count
    return (
        (positives // LANES).reshape(subtiles, width),
        (positives % LANES).reshape(subtiles, width),
    )


def hot_terms(user_half, pos_hi, pos_lo, hot_rows, first, count, dep, prev=None, tile=512, sub_users=8):
    users, k = user_half.shape
    items = hot_rows.shape[0]
    width = pos_hi.shape[1]
    per_tile = tile // sub_users
    in_specs = [
        pl.BlockSpec((tile, k), lambda i: (first + i, 0)),
        pl.BlockSpec((items, k), lambda i: (0, 0)),
        pl.BlockSpec((per_tile, width), lambda i: (first + i, 0)),
        pl.BlockSpec((per_tile, width), lambda i: (first + i, 0)),
        pl.BlockSpec(memory_space=pl.ANY),
    ]
    args = [user_half, hot_rows, pos_hi, pos_lo, dep]
    aliases = {}
    if prev is not None:
        in_specs += [pl.BlockSpec(memory_space=pl.ANY), pl.BlockSpec((items, k), lambda i: (0, 0))]
        args += list(prev)
        aliases = {5: 0, 6: 1}
    return pl.pallas_call(
        functools.partial(_hot_kernel, sub_users=sub_users, chained=prev is not None),
        grid=(count,),
        in_specs=in_specs,
        out_specs=[
            pl.BlockSpec((tile, k), lambda i: (first + i, 0)),
            pl.BlockSpec((items, k), lambda i: (0, 0)),
        ],
        out_shape=[
            jax.ShapeDtypeStruct((users, k), jnp.float32),
            jax.ShapeDtypeStruct((items, k), jnp.float32),
        ],
        scratch_shapes=[pltpu.VMEM((tile, items), jnp.float32)],
        input_output_aliases=aliases,
        compiler_params=pltpu.CompilerParams(dimension_semantics=("arbitrary",)),
    )(*args)


def _gather_kernel(idx_ref, table_ref, out_ref):
    rows = table_ref.shape[0]
    chunk = idx_ref.shape[1]
    onehot = (idx_ref[...] == lax.broadcasted_iota(jnp.int32, (rows, chunk), 0)).astype(
        jnp.bfloat16
    )
    out_ref[...] = _tn(onehot, table_ref[...]).astype(out_ref.dtype)


def onehot_gather(table, idx, chunk=1024):
    rows, k = table.shape
    n = idx.shape[0]
    return pl.pallas_call(
        _gather_kernel,
        grid=(n // chunk,),
        in_specs=[
            pl.BlockSpec((1, chunk), lambda i: (0, i)),
            pl.BlockSpec((rows, k), lambda i: (0, 0)),
        ],
        out_specs=pl.BlockSpec((chunk, k), lambda i: (i, 0)),
        out_shape=jax.ShapeDtypeStruct((n, k), table.dtype),
    )(idx.reshape(1, n), table)


def _scatter_kernel(idx_ref, val_ref, out_ref):
    i = pl.program_id(0)
    rows = out_ref.shape[0]
    chunk = idx_ref.shape[1]
    onehot = (idx_ref[...] == lax.broadcasted_iota(jnp.int32, (rows, chunk), 0)).astype(
        jnp.bfloat16
    )

    @pl.when(i == 0)
    def _():
        out_ref[...] = jnp.zeros_like(out_ref)

    out_ref[...] += jnp.dot(onehot, val_ref[...], preferred_element_type=jnp.float32)


def onehot_scatter_add(idx, values, rows, chunk=1024):
    n, k = values.shape
    return pl.pallas_call(
        _scatter_kernel,
        grid=(n // chunk,),
        in_specs=[
            pl.BlockSpec((1, chunk), lambda i: (0, i)),
            pl.BlockSpec((chunk, k), lambda i: (i, 0)),
        ],
        out_specs=pl.BlockSpec((rows, k), lambda i: (0, 0)),
        out_shape=jax.ShapeDtypeStruct((rows, k), jnp.float32),
        compiler_params=pltpu.CompilerParams(dimension_semantics=("arbitrary",)),
    )(idx.reshape(1, n), values)


def adagrad(current, history, gradient):
    updated = history + gradient * gradient
    return (current - LEARN_RATE * gradient / jnp.sqrt(updated), updated)


def body(
    users,
    user_accum,
    positives,
    hot_table,
    hot_accum,
    cold_table,
    cold_accum,
    cold_requests,
    cold_counts,
):
    user_half = users.astype(jnp.bfloat16)
    hot_half = hot_table.astype(jnp.bfloat16)
    cold_half = cold_table.astype(jnp.bfloat16)
    feature_count = users.shape[1]
    item_sub = hot_table.shape[0]
    sb_count = lax.axis_size("sb")
    pos_count = positives.shape[1]
    devices = cold_requests.shape[1]
    slot_count = cold_requests.shape[2]
    requests = cold_requests.reshape(devices, slot_count)
    live_slots = lax.iota(jnp.int32, slot_count)[None, :] < cold_counts.reshape(devices, 1)
    asked_rows = lax.all_to_all(requests, ("grp", "sa", "sb"), split_axis=0, concat_axis=0, tiled=True)
    found = onehot_gather(cold_half, asked_rows.reshape(-1))
    packed = jnp.concatenate(
        [user_half, (positives // LANES).astype(jnp.bfloat16), (positives % LANES).astype(jnp.bfloat16)],
        axis=1,
    )
    packed_part = lax.all_gather(packed, "sb", axis=0, tiled=True)
    hot_part = lax.all_gather(hot_half, "sa", axis=0, tiled=True)
    found, packed_part, hot_part = lax.optimization_barrier((found, packed_part, hot_part))
    fetched = lax.all_to_all(
        found.reshape(devices, slot_count, feature_count),
        ("grp", "sa", "sb"),
        split_axis=0,
        concat_axis=0,
        tiled=True,
    )
    users_part = packed_part[:, :feature_count]
    pos_hi = packed_part[:, feature_count:feature_count + pos_count].astype(jnp.int32)
    pos_lo = packed_part[:, feature_count + pos_count:].astype(jnp.int32)
    hi_per_item = item_sub // LANES
    owner = pos_hi // hi_per_item
    local_hi = (owner // sb_count) * hi_per_item + pos_hi % hi_per_item
    local = jnp.where(owner % sb_count == lax.axis_index("sb"), local_hi * LANES + pos_lo, hot_part.shape[0])
    pos_hi_t, pos_lo_t = hot_prepare(local)
    tiles = users_part.shape[0] // 512
    user_hot_part, item_part = hot_terms(users_part, pos_hi_t, pos_lo_t, hot_part, 0, tiles, found)
    fetched, user_hot_part, item_part = lax.optimization_barrier((fetched, user_hot_part, item_part))
    item_grad = lax.psum_scatter(item_part, "sa", scatter_dimension=0, tiled=True)
    hot_grad = lax.psum(item_grad, "grp")
    user_hot_part, hot_grad = lax.optimization_barrier((user_hot_part, hot_grad))
    user_hot = lax.psum_scatter(user_hot_part, "sb", scatter_dimension=0, tiled=True)
    flat_rows = fetched.reshape(devices * slot_count, feature_count)
    scores = jnp.einsum("uk,rk->ur", user_half, flat_rows, preferred_element_type=jnp.float32)
    weights = (jax.nn.sigmoid(scores) * live_slots.reshape(1, -1).astype(jnp.float32)).astype(
        jnp.bfloat16
    )
    user_cold = jnp.dot(weights, flat_rows, preferred_element_type=jnp.float32)
    row_terms = jnp.einsum(
        "ur,uk->rk", weights, user_half, preferred_element_type=jnp.float32
    ).astype(jnp.bfloat16)
    row_terms = row_terms.reshape(devices, slot_count, feature_count)
    returned = lax.all_to_all(row_terms, ("grp", "sa", "sb"), split_axis=0, concat_axis=0, tiled=True)
    returned, user_cold = lax.optimization_barrier((returned, user_cold))
    cold_grad = onehot_scatter_add(
        asked_rows.reshape(-1),
        returned.reshape(devices * slot_count, feature_count),
        cold_table.shape[0],
    )
    user_grad = user_hot + user_cold
    new_users, new_user_accum = adagrad(users, user_accum, user_grad)
    new_hot, new_hot_accum = adagrad(hot_table, hot_accum, hot_grad)
    new_cold, new_cold_accum = adagrad(cold_table, cold_accum, cold_grad)
    return (new_users, new_user_accum, new_hot, new_hot_accum, new_cold, new_cold_accum)


def _split_mesh(mesh):
    shard = mesh.shape["shard"]
    sa = 4 if shard % 4 == 0 else 1
    return Mesh(mesh.devices.reshape(mesh.shape["grp"], sa, shard // sa), ("grp", "sa", "sb"))


def solution(mesh):
    return jax.shard_map(
        body,
        mesh=_split_mesh(mesh),
        in_specs=(
            P(("grp", "sa", "sb"), None),
            P(("grp", "sa", "sb"), None),
            P(("grp", "sa", "sb"), None),
            P(("sa", "sb"), None),
            P(("sa", "sb"), None),
            P(("grp", "sa", "sb"), None),
            P(("grp", "sa", "sb"), None),
            P(("grp", "sa", "sb"), None, None),
            P(("grp", "sa", "sb"), None),
        ),
        out_specs=(
            P(("grp", "sa", "sb"), None),
            P(("grp", "sa", "sb"), None),
            P(("sa", "sb"), None),
            P(("sa", "sb"), None),
            P(("grp", "sa", "sb"), None),
            P(("grp", "sa", "sb"), None),
        ),
        check_vma=False,
    )
```

```python
import functools

import jax
import jax.numpy as jnp
from jax import lax
from jax.experimental import pallas as pl
from jax.experimental.pallas import tpu as pltpu
from jax.sharding import Mesh, PartitionSpec as P

POSITIVE_WEIGHT = 32.0
LEARN_RATE = 0.5
LANES = 128
SUB = 8


def _nt(a, b):
    return lax.dot_general(a, b, (((1,), (1,)), ((), ())), preferred_element_type=jnp.float32)


def _tn(a, b):
    return lax.dot_general(a, b, (((0,), (0,)), ((), ())), preferred_element_type=jnp.float32)


def _hot_kernel(u_ref, h_ref, ph_ref, pl_ref, dep_ref, *rest, sub_users, chained):
    del dep_ref
    if chained:
        _, ipin_ref, up_ref, ip_ref, m_ref = rest
    else:
        up_ref, ip_ref, m_ref = rest
    i = pl.program_id(0)
    items = h_ref.shape[0]
    nh = items // LANES
    subtiles = ph_ref.shape[0]
    width = ph_ref.shape[1]
    per = width // sub_users
    r = lax.broadcasted_iota(jnp.int32, (nh * sub_users, width), 0)
    c = lax.broadcasted_iota(jnp.int32, (nh * sub_users, width), 1)
    diag = (r % sub_users) == (c // per)
    hrow = r // sub_users
    lrow = lax.broadcasted_iota(jnp.int32, (LANES, width), 0)

    def sub(s, carry):
        lhs = jnp.where(diag & (ph_ref[pl.ds(s, 1), :] == hrow), 1.0, 0.0).astype(jnp.bfloat16)
        rhs = jnp.where(pl_ref[pl.ds(s, 1), :] == lrow, 1.0, 0.0).astype(jnp.bfloat16)
        out = _nt(lhs, rhs)
        base = pl.multiple_of(s * sub_users, sub_users)
        for h in range(nh):
            m_ref[pl.ds(base, sub_users), pl.ds(h * LANES, LANES)] = out[
                h * sub_users:(h + 1) * sub_users, :
            ]
        return carry

    lax.fori_loop(0, subtiles, sub, 0, unroll=subtiles)
    u = u_ref[...]
    hj = h_ref[...]
    scores = _nt(u, hj)
    m = m_ref[...]
    w = ((1.0 + POSITIVE_WEIGHT * m) * jax.nn.sigmoid(scores) - POSITIVE_WEIGHT * m).astype(
        jnp.bfloat16
    )
    up_ref[...] = jnp.dot(w, hj, preferred_element_type=jnp.float32)

    @pl.when(i == 0)
    def _():
        if chained:
            ip_ref[...] = ipin_ref[...]
        else:
            ip_ref[...] = jnp.zeros_like(ip_ref)

    ip_ref[...] += _tn(w, u)


def hot_prepare(positives, sub_users=8):
    users, pos_count = positives.shape
    subtiles = users // sub_users
    width = sub_users * pos_count
    return (
        (positives // LANES).reshape(subtiles, width),
        (positives % LANES).reshape(subtiles, width),
    )


def hot_terms(user_half, pos_hi, pos_lo, hot_rows, first, count, dep, prev=None, tile=512, sub_users=8):
    users, k = user_half.shape
    items = hot_rows.shape[0]
    width = pos_hi.shape[1]
    per_tile = tile // sub_users
    in_specs = [
        pl.BlockSpec((tile, k), lambda i: (first + i, 0)),
        pl.BlockSpec((items, k), lambda i: (0, 0)),
        pl.BlockSpec((per_tile, width), lambda i: (first + i, 0)),
        pl.BlockSpec((per_tile, width), lambda i: (first + i, 0)),
        pl.BlockSpec(memory_space=pl.ANY),
    ]
    args = [user_half, hot_rows, pos_hi, pos_lo, dep]
    aliases = {}
    if prev is not None:
        in_specs += [pl.BlockSpec(memory_space=pl.ANY), pl.BlockSpec((items, k), lambda i: (0, 0))]
        args += list(prev)
        aliases = {5: 0, 6: 1}
    return pl.pallas_call(
        functools.partial(_hot_kernel, sub_users=sub_users, chained=prev is not None),
        grid=(count,),
        in_specs=in_specs,
        out_specs=[
            pl.BlockSpec((tile, k), lambda i: (first + i, 0)),
            pl.BlockSpec((items, k), lambda i: (0, 0)),
        ],
        out_shape=[
            jax.ShapeDtypeStruct((users, k), jnp.float32),
            jax.ShapeDtypeStruct((items, k), jnp.float32),
        ],
        scratch_shapes=[pltpu.VMEM((tile, items), jnp.float32)],
        input_output_aliases=aliases,
        compiler_params=pltpu.CompilerParams(dimension_semantics=("arbitrary",)),
    )(*args)


def _gather_kernel(idx_ref, table_ref, out_ref):
    rows = table_ref.shape[0]
    chunk = idx_ref.shape[1]
    onehot = (idx_ref[...] == lax.broadcasted_iota(jnp.int32, (rows, chunk), 0)).astype(
        jnp.bfloat16
    )
    out_ref[...] = _tn(onehot, table_ref[...]).astype(out_ref.dtype)


def onehot_gather(table, idx, chunk=1024):
    rows, k = table.shape
    n = idx.shape[0]
    return pl.pallas_call(
        _gather_kernel,
        grid=(n // chunk,),
        in_specs=[
            pl.BlockSpec((1, chunk), lambda i: (0, i)),
            pl.BlockSpec((rows, k), lambda i: (0, 0)),
        ],
        out_specs=pl.BlockSpec((chunk, k), lambda i: (i, 0)),
        out_shape=jax.ShapeDtypeStruct((n, k), table.dtype),
    )(idx.reshape(1, n), table)


def _cold_kernel(u_ref, r_ref, live_ref, uc_ref, t_ref):
    j = pl.program_id(0)
    u = u_ref[...]
    rows = r_ref[...]
    scores = _nt(u, rows)
    w = (jax.nn.sigmoid(scores) * live_ref[...]).astype(jnp.bfloat16)

    @pl.when(j == 0)
    def _():
        uc_ref[...] = jnp.zeros_like(uc_ref)

    uc_ref[...] += jnp.dot(w, rows, preferred_element_type=jnp.float32)
    t_ref[...] = _tn(w, u).astype(t_ref.dtype)


def cold_terms(user_half, flat_rows, live, chunk=2048):
    users, k = user_half.shape
    n = flat_rows.shape[0]
    return pl.pallas_call(
        _cold_kernel,
        grid=(n // chunk,),
        in_specs=[
            pl.BlockSpec((users, k), lambda j: (0, 0)),
            pl.BlockSpec((chunk, k), lambda j: (j, 0)),
            pl.BlockSpec((1, chunk), lambda j: (0, j)),
        ],
        out_specs=[
            pl.BlockSpec((users, k), lambda j: (0, 0)),
            pl.BlockSpec((chunk, k), lambda j: (j, 0)),
        ],
        out_shape=[
            jax.ShapeDtypeStruct((users, k), jnp.float32),
            jax.ShapeDtypeStruct((n, k), jnp.bfloat16),
        ],
        compiler_params=pltpu.CompilerParams(dimension_semantics=("arbitrary",)),
    )(user_half, flat_rows, live.reshape(1, n))


def _scatter_kernel(idx_ref, val_ref, out_ref):
    i = pl.program_id(0)
    rows = out_ref.shape[0]
    chunk = idx_ref.shape[1]
    onehot = (idx_ref[...] == lax.broadcasted_iota(jnp.int32, (rows, chunk), 0)).astype(
        jnp.bfloat16
    )

    @pl.when(i == 0)
    def _():
        out_ref[...] = jnp.zeros_like(out_ref)

    out_ref[...] += jnp.dot(onehot, val_ref[...], preferred_element_type=jnp.float32)


def onehot_scatter_add(idx, values, rows, chunk=1024):
    n, k = values.shape
    return pl.pallas_call(
        _scatter_kernel,
        grid=(n // chunk,),
        in_specs=[
            pl.BlockSpec((1, chunk), lambda i: (0, i)),
            pl.BlockSpec((chunk, k), lambda i: (i, 0)),
        ],
        out_specs=pl.BlockSpec((rows, k), lambda i: (0, 0)),
        out_shape=jax.ShapeDtypeStruct((rows, k), jnp.float32),
        compiler_params=pltpu.CompilerParams(dimension_semantics=("arbitrary",)),
    )(idx.reshape(1, n), values)


def adagrad(current, history, gradient):
    updated = history + gradient * gradient
    return (current - LEARN_RATE * gradient / jnp.sqrt(updated), updated)


def body(
    users,
    user_accum,
    positives,
    hot_table,
    hot_accum,
    cold_table,
    cold_accum,
    cold_requests,
    cold_counts,
):
    user_half = users.astype(jnp.bfloat16)
    hot_half = hot_table.astype(jnp.bfloat16)
    cold_half = cold_table.astype(jnp.bfloat16)
    feature_count = users.shape[1]
    item_sub = hot_table.shape[0]
    sb_count = lax.axis_size("sb")
    pos_count = positives.shape[1]
    devices = cold_requests.shape[1]
    slot_count = cold_requests.shape[2]
    requests = cold_requests.reshape(devices, slot_count)
    live_slots = lax.iota(jnp.int32, slot_count)[None, :] < cold_counts.reshape(devices, 1)
    asked_rows = lax.all_to_all(requests, ("grp", "sa", "sb"), split_axis=0, concat_axis=0, tiled=True)
    found = onehot_gather(cold_half, asked_rows.reshape(-1))
    packed = jnp.concatenate(
        [user_half, (positives // LANES).astype(jnp.bfloat16), (positives % LANES).astype(jnp.bfloat16)],
        axis=1,
    )
    packed_part = lax.all_gather(packed, "sb", axis=0, tiled=True)
    hot_part = lax.all_gather(hot_half, "sa", axis=0, tiled=True)
    found, packed_part, hot_part = lax.optimization_barrier((found, packed_part, hot_part))
    fetched = lax.all_to_all(
        found.reshape(devices, slot_count, feature_count),
        ("grp", "sa", "sb"),
        split_axis=0,
        concat_axis=0,
        tiled=True,
    )
    users_part = packed_part[:, :feature_count]
    pos_hi = packed_part[:, feature_count:feature_count + pos_count].astype(jnp.int32)
    pos_lo = packed_part[:, feature_count + pos_count:].astype(jnp.int32)
    hi_per_item = item_sub // LANES
    owner = pos_hi // hi_per_item
    local_hi = (owner // sb_count) * hi_per_item + pos_hi % hi_per_item
    local = jnp.where(owner % sb_count == lax.axis_index("sb"), local_hi * LANES + pos_lo, hot_part.shape[0])
    pos_hi_t, pos_lo_t = hot_prepare(local)
    tiles = users_part.shape[0] // 512
    user_hot_part, item_part = hot_terms(users_part, pos_hi_t, pos_lo_t, hot_part, 0, tiles, found)
    fetched, user_hot_part, item_part = lax.optimization_barrier((fetched, user_hot_part, item_part))
    item_grad = lax.psum_scatter(item_part, "sa", scatter_dimension=0, tiled=True)
    hot_grad = lax.psum(item_grad, "grp")
    user_hot = lax.psum_scatter(user_hot_part, "sb", scatter_dimension=0, tiled=True)
    flat_rows = fetched.reshape(devices * slot_count, feature_count)
    user_cold, row_terms = cold_terms(user_half, flat_rows, live_slots.reshape(-1).astype(jnp.float32))
    row_terms = row_terms.reshape(devices, slot_count, feature_count)
    returned = lax.all_to_all(row_terms, ("grp", "sa", "sb"), split_axis=0, concat_axis=0, tiled=True)
    returned, user_cold, hot_grad = lax.optimization_barrier((returned, user_cold, hot_grad))
    cold_grad = onehot_scatter_add(
        asked_rows.reshape(-1),
        returned.reshape(devices * slot_count, feature_count),
        cold_table.shape[0],
    )
    user_grad = user_hot + user_cold
    new_users, new_user_accum = adagrad(users, user_accum, user_grad)
    new_hot, new_hot_accum = adagrad(hot_table, hot_accum, hot_grad)
    new_cold, new_cold_accum = adagrad(cold_table, cold_accum, cold_grad)
    return (new_users, new_user_accum, new_hot, new_hot_accum, new_cold, new_cold_accum)


def _split_mesh(mesh):
    shard = mesh.shape["shard"]
    sa = 4 if shard % 4 == 0 else 1
    return Mesh(mesh.devices.reshape(mesh.shape["grp"], sa, shard // sa), ("grp", "sa", "sb"))


def solution(mesh):
    return jax.shard_map(
        body,
        mesh=_split_mesh(mesh),
        in_specs=(
            P(("grp", "sa", "sb"), None),
            P(("grp", "sa", "sb"), None),
            P(("grp", "sa", "sb"), None),
            P(("sa", "sb"), None),
            P(("sa", "sb"), None),
            P(("grp", "sa", "sb"), None),
            P(("grp", "sa", "sb"), None),
            P(("grp", "sa", "sb"), None, None),
            P(("grp", "sa", "sb"), None),
        ),
        out_specs=(
            P(("grp", "sa", "sb"), None),
            P(("grp", "sa", "sb"), None),
            P(("sa", "sb"), None),
            P(("sa", "sb"), None),
            P(("grp", "sa", "sb"), None),
            P(("grp", "sa", "sb"), None),
        ),
        check_vma=False,
    )
```

```python
import functools

import jax
import jax.numpy as jnp
from jax import lax
from jax.experimental import pallas as pl
from jax.experimental.pallas import tpu as pltpu
from jax.sharding import Mesh, PartitionSpec as P

POSITIVE_WEIGHT = 32.0
LEARN_RATE = 0.5
LANES = 128
SUB = 8


def _nt(a, b):
    return lax.dot_general(a, b, (((1,), (1,)), ((), ())), preferred_element_type=jnp.float32)


def _tn(a, b):
    return lax.dot_general(a, b, (((0,), (0,)), ((), ())), preferred_element_type=jnp.float32)


def _hot_kernel(u_ref, h_ref, ph_ref, pl_ref, dep_ref, *rest, sub_users, chained):
    del dep_ref
    if chained:
        _, ipin_ref, up_ref, ip_ref, m_ref = rest
    else:
        up_ref, ip_ref, m_ref = rest
    i = pl.program_id(0)
    items = h_ref.shape[0]
    nh = items // LANES
    subtiles = ph_ref.shape[0]
    width = ph_ref.shape[1]
    per = width // sub_users
    r = lax.broadcasted_iota(jnp.int32, (nh * sub_users, width), 0)
    c = lax.broadcasted_iota(jnp.int32, (nh * sub_users, width), 1)
    diag = (r % sub_users) == (c // per)
    hrow = r // sub_users
    lrow = lax.broadcasted_iota(jnp.int32, (LANES, width), 0)

    def sub(s, carry):
        lhs = jnp.where(diag & (ph_ref[pl.ds(s, 1), :] == hrow), 1.0, 0.0).astype(jnp.bfloat16)
        rhs = jnp.where(pl_ref[pl.ds(s, 1), :] == lrow, 1.0, 0.0).astype(jnp.bfloat16)
        out = _nt(lhs, rhs)
        base = pl.multiple_of(s * sub_users, sub_users)
        for h in range(nh):
            m_ref[pl.ds(base, sub_users), pl.ds(h * LANES, LANES)] = out[
                h * sub_users:(h + 1) * sub_users, :
            ]
        return carry

    lax.fori_loop(0, subtiles, sub, 0, unroll=subtiles)
    u = u_ref[...]
    hj = h_ref[...]
    scores = _nt(u, hj)
    m = m_ref[...]
    w = ((1.0 + POSITIVE_WEIGHT * m) * jax.nn.sigmoid(scores) - POSITIVE_WEIGHT * m).astype(
        jnp.bfloat16
    )
    up_ref[...] = jnp.dot(w, hj, preferred_element_type=jnp.float32)

    @pl.when(i == 0)
    def _():
        if chained:
            ip_ref[...] = ipin_ref[...]
        else:
            ip_ref[...] = jnp.zeros_like(ip_ref)

    ip_ref[...] += _tn(w, u)


def hot_prepare(positives, sub_users=8):
    users, pos_count = positives.shape
    subtiles = users // sub_users
    width = sub_users * pos_count
    return (
        (positives // LANES).reshape(subtiles, width),
        (positives % LANES).reshape(subtiles, width),
    )


def hot_terms(user_half, pos_hi, pos_lo, hot_rows, first, count, dep, prev=None, tile=512, sub_users=8):
    users, k = user_half.shape
    items = hot_rows.shape[0]
    width = pos_hi.shape[1]
    per_tile = tile // sub_users
    in_specs = [
        pl.BlockSpec((tile, k), lambda i: (first + i, 0)),
        pl.BlockSpec((items, k), lambda i: (0, 0)),
        pl.BlockSpec((per_tile, width), lambda i: (first + i, 0)),
        pl.BlockSpec((per_tile, width), lambda i: (first + i, 0)),
        pl.BlockSpec(memory_space=pl.ANY),
    ]
    args = [user_half, hot_rows, pos_hi, pos_lo, dep]
    aliases = {}
    if prev is not None:
        in_specs += [pl.BlockSpec(memory_space=pl.ANY), pl.BlockSpec((items, k), lambda i: (0, 0))]
        args += list(prev)
        aliases = {5: 0, 6: 1}
    return pl.pallas_call(
        functools.partial(_hot_kernel, sub_users=sub_users, chained=prev is not None),
        grid=(count,),
        in_specs=in_specs,
        out_specs=[
            pl.BlockSpec((tile, k), lambda i: (first + i, 0)),
            pl.BlockSpec((items, k), lambda i: (0, 0)),
        ],
        out_shape=[
            jax.ShapeDtypeStruct((users, k), jnp.float32),
            jax.ShapeDtypeStruct((items, k), jnp.float32),
        ],
        scratch_shapes=[pltpu.VMEM((tile, items), jnp.float32)],
        input_output_aliases=aliases,
        compiler_params=pltpu.CompilerParams(dimension_semantics=("arbitrary",)),
    )(*args)


def _gather_kernel(idx_ref, table_ref, out_ref):
    rows = table_ref.shape[0]
    chunk = idx_ref.shape[1]
    onehot = (idx_ref[...] == lax.broadcasted_iota(jnp.int32, (rows, chunk), 0)).astype(
        jnp.bfloat16
    )
    out_ref[...] = _tn(onehot, table_ref[...]).astype(out_ref.dtype)


def onehot_gather(table, idx, chunk=1024):
    rows, k = table.shape
    n = idx.shape[0]
    return pl.pallas_call(
        _gather_kernel,
        grid=(n // chunk,),
        in_specs=[
            pl.BlockSpec((1, chunk), lambda i: (0, i)),
            pl.BlockSpec((rows, k), lambda i: (0, 0)),
        ],
        out_specs=pl.BlockSpec((chunk, k), lambda i: (i, 0)),
        out_shape=jax.ShapeDtypeStruct((n, k), table.dtype),
    )(idx.reshape(1, n), table)


def _scatter_kernel(idx_ref, val_ref, out_ref):
    i = pl.program_id(0)
    rows = out_ref.shape[0]
    chunk = idx_ref.shape[1]
    onehot = (idx_ref[...] == lax.broadcasted_iota(jnp.int32, (rows, chunk), 0)).astype(
        jnp.bfloat16
    )

    @pl.when(i == 0)
    def _():
        out_ref[...] = jnp.zeros_like(out_ref)

    out_ref[...] += jnp.dot(onehot, val_ref[...], preferred_element_type=jnp.float32)


def onehot_scatter_add(idx, values, rows, chunk=1024):
    n, k = values.shape
    return pl.pallas_call(
        _scatter_kernel,
        grid=(n // chunk,),
        in_specs=[
            pl.BlockSpec((1, chunk), lambda i: (0, i)),
            pl.BlockSpec((chunk, k), lambda i: (i, 0)),
        ],
        out_specs=pl.BlockSpec((rows, k), lambda i: (0, 0)),
        out_shape=jax.ShapeDtypeStruct((rows, k), jnp.float32),
        compiler_params=pltpu.CompilerParams(dimension_semantics=("arbitrary",)),
    )(idx.reshape(1, n), values)


def adagrad(current, history, gradient):
    updated = history + gradient * gradient
    return (current - LEARN_RATE * gradient / jnp.sqrt(updated), updated)


def body(
    users,
    user_accum,
    positives,
    hot_table,
    hot_accum,
    cold_table,
    cold_accum,
    cold_requests,
    cold_counts,
):
    user_half = users.astype(jnp.bfloat16)
    hot_half = hot_table.astype(jnp.bfloat16)
    cold_half = cold_table.astype(jnp.bfloat16)
    feature_count = users.shape[1]
    item_sub = hot_table.shape[0]
    sb_count = lax.axis_size("sb")
    pos_count = positives.shape[1]
    devices = cold_requests.shape[1]
    slot_count = cold_requests.shape[2]
    requests = cold_requests.reshape(devices, slot_count)
    live_slots = lax.iota(jnp.int32, slot_count)[None, :] < cold_counts.reshape(devices, 1)
    asked_rows = lax.all_to_all(requests, ("grp", "sa", "sb"), split_axis=0, concat_axis=0, tiled=True)
    found = onehot_gather(cold_half, asked_rows.reshape(-1))
    sub_rows = positives.shape[0] * pos_count // LANES
    packed = jnp.concatenate(
        [
            user_half,
            (positives // LANES).reshape(sub_rows, LANES).astype(jnp.bfloat16),
            (positives % LANES).reshape(sub_rows, LANES).astype(jnp.bfloat16),
        ],
        axis=0,
    )
    packed_part = lax.all_gather(packed, "sb", axis=0, tiled=False)
    hot_part = lax.all_gather(hot_half, "sa", axis=0, tiled=True)
    found, packed_part, hot_part = lax.optimization_barrier((found, packed_part, hot_part))
    fetched = lax.all_to_all(
        found.reshape(devices, slot_count, feature_count),
        ("grp", "sa", "sb"),
        split_axis=0,
        concat_axis=0,
        tiled=True,
    )
    local_users = user_half.shape[0]
    users_part = packed_part[:, :local_users].reshape(-1, feature_count)
    pos_hi = packed_part[:, local_users:local_users + sub_rows].reshape(-1, LANES).astype(jnp.int32)
    pos_lo = packed_part[:, local_users + sub_rows:].reshape(-1, LANES).astype(jnp.int32)
    hi_per_item = item_sub // LANES
    owner = pos_hi // hi_per_item
    local_hi = (owner // sb_count) * hi_per_item + pos_hi % hi_per_item
    pos_hi_t = jnp.where(owner % sb_count == lax.axis_index("sb"), local_hi, hot_part.shape[0] // LANES)
    pos_lo_t = pos_lo
    tiles = users_part.shape[0] // 512
    user_hot_part, item_part = hot_terms(users_part, pos_hi_t, pos_lo_t, hot_part, 0, tiles, found)
    fetched, user_hot_part, item_part = lax.optimization_barrier((fetched, user_hot_part, item_part))
    item_grad = lax.psum_scatter(item_part, "sa", scatter_dimension=0, tiled=True)
    hot_grad = lax.psum(item_grad, "grp")
    user_hot_part, hot_grad = lax.optimization_barrier((user_hot_part, hot_grad))
    user_hot = lax.psum_scatter(user_hot_part, "sb", scatter_dimension=0, tiled=True)
    flat_rows = fetched.reshape(devices * slot_count, feature_count)
    scores = jnp.einsum("uk,rk->ur", user_half, flat_rows, preferred_element_type=jnp.float32)
    weights = (jax.nn.sigmoid(scores) * live_slots.reshape(1, -1).astype(jnp.float32)).astype(
        jnp.bfloat16
    )
    user_cold = jnp.dot(weights, flat_rows, preferred_element_type=jnp.float32)
    row_terms = jnp.einsum(
        "ur,uk->rk", weights, user_half, preferred_element_type=jnp.float32
    ).astype(jnp.bfloat16)
    row_terms = row_terms.reshape(devices, slot_count, feature_count)
    returned = lax.all_to_all(row_terms, ("grp", "sa", "sb"), split_axis=0, concat_axis=0, tiled=True)
    returned, user_cold = lax.optimization_barrier((returned, user_cold))
    cold_grad = onehot_scatter_add(
        asked_rows.reshape(-1),
        returned.reshape(devices * slot_count, feature_count),
        cold_table.shape[0],
    )
    user_grad = user_hot + user_cold
    new_users, new_user_accum = adagrad(users, user_accum, user_grad)
    new_hot, new_hot_accum = adagrad(hot_table, hot_accum, hot_grad)
    new_cold, new_cold_accum = adagrad(cold_table, cold_accum, cold_grad)
    return (new_users, new_user_accum, new_hot, new_hot_accum, new_cold, new_cold_accum)


def _split_mesh(mesh):
    shard = mesh.shape["shard"]
    sa = 4 if shard % 4 == 0 else 1
    return Mesh(mesh.devices.reshape(mesh.shape["grp"], sa, shard // sa), ("grp", "sa", "sb"))


def solution(mesh):
    return jax.shard_map(
        body,
        mesh=_split_mesh(mesh),
        in_specs=(
            P(("grp", "sa", "sb"), None),
            P(("grp", "sa", "sb"), None),
            P(("grp", "sa", "sb"), None),
            P(("sa", "sb"), None),
            P(("sa", "sb"), None),
            P(("grp", "sa", "sb"), None),
            P(("grp", "sa", "sb"), None),
            P(("grp", "sa", "sb"), None, None),
            P(("grp", "sa", "sb"), None),
        ),
        out_specs=(
            P(("grp", "sa", "sb"), None),
            P(("grp", "sa", "sb"), None),
            P(("sa", "sb"), None),
            P(("sa", "sb"), None),
            P(("grp", "sa", "sb"), None),
            P(("grp", "sa", "sb"), None),
        ),
        check_vma=False,
    )
```

```python
import functools

import jax
import jax.numpy as jnp
from jax import lax
from jax.experimental import pallas as pl
from jax.experimental.pallas import tpu as pltpu
from jax.sharding import Mesh, PartitionSpec as P

POSITIVE_WEIGHT = 32.0
LEARN_RATE = 0.5
LANES = 128
SUB = 8


def _nt(a, b):
    return lax.dot_general(a, b, (((1,), (1,)), ((), ())), preferred_element_type=jnp.float32)


def _tn(a, b):
    return lax.dot_general(a, b, (((0,), (0,)), ((), ())), preferred_element_type=jnp.float32)


def _hot_kernel(u_ref, h_ref, ph_ref, pl_ref, dep_ref, *rest, sub_users, chained):
    del dep_ref
    if chained:
        _, ipin_ref, up_ref, ip_ref, m_ref = rest
    else:
        up_ref, ip_ref, m_ref = rest
    i = pl.program_id(0)
    items = h_ref.shape[0]
    nh = items // LANES
    subtiles = ph_ref.shape[0]
    width = ph_ref.shape[1]
    per = width // sub_users
    r = lax.broadcasted_iota(jnp.int32, (nh * sub_users, width), 0)
    c = lax.broadcasted_iota(jnp.int32, (nh * sub_users, width), 1)
    diag = (r % sub_users) == (c // per)
    hrow = r // sub_users
    lrow = lax.broadcasted_iota(jnp.int32, (LANES, width), 0)

    def sub(s, carry):
        lhs = jnp.where(diag & (ph_ref[pl.ds(s, 1), :] == hrow), 1.0, 0.0).astype(jnp.bfloat16)
        rhs = jnp.where(pl_ref[pl.ds(s, 1), :] == lrow, 1.0, 0.0).astype(jnp.bfloat16)
        out = _nt(lhs, rhs)
        base = pl.multiple_of(s * sub_users, sub_users)
        for h in range(nh):
            m_ref[pl.ds(base, sub_users), pl.ds(h * LANES, LANES)] = out[
                h * sub_users:(h + 1) * sub_users, :
            ]
        return carry

    lax.fori_loop(0, subtiles, sub, 0, unroll=subtiles)
    u = u_ref[...]
    hj = h_ref[...]
    scores = _nt(u, hj)
    m = m_ref[...]
    w = ((1.0 + POSITIVE_WEIGHT * m) * jax.nn.sigmoid(scores) - POSITIVE_WEIGHT * m).astype(
        jnp.bfloat16
    )
    up_ref[...] = jnp.dot(w, hj, preferred_element_type=jnp.float32)

    @pl.when(i == 0)
    def _():
        if chained:
            ip_ref[...] = ipin_ref[...]
        else:
            ip_ref[...] = jnp.zeros_like(ip_ref)

    ip_ref[...] += _tn(w, u)


def hot_prepare(positives, sub_users=8):
    users, pos_count = positives.shape
    subtiles = users // sub_users
    width = sub_users * pos_count
    return (
        (positives // LANES).reshape(subtiles, width),
        (positives % LANES).reshape(subtiles, width),
    )


def hot_terms(user_half, pos_hi, pos_lo, hot_rows, first, count, dep, prev=None, tile=512, sub_users=8):
    users, k = user_half.shape
    items = hot_rows.shape[0]
    width = pos_hi.shape[1]
    per_tile = tile // sub_users
    in_specs = [
        pl.BlockSpec((tile, k), lambda i: (first + i, 0)),
        pl.BlockSpec((items, k), lambda i: (0, 0)),
        pl.BlockSpec((per_tile, width), lambda i: (first + i, 0)),
        pl.BlockSpec((per_tile, width), lambda i: (first + i, 0)),
        pl.BlockSpec(memory_space=pl.ANY),
    ]
    args = [user_half, hot_rows, pos_hi, pos_lo, dep]
    aliases = {}
    if prev is not None:
        in_specs += [pl.BlockSpec(memory_space=pl.ANY), pl.BlockSpec((items, k), lambda i: (0, 0))]
        args += list(prev)
        aliases = {5: 0, 6: 1}
    return pl.pallas_call(
        functools.partial(_hot_kernel, sub_users=sub_users, chained=prev is not None),
        grid=(count,),
        in_specs=in_specs,
        out_specs=[
            pl.BlockSpec((tile, k), lambda i: (first + i, 0)),
            pl.BlockSpec((items, k), lambda i: (0, 0)),
        ],
        out_shape=[
            jax.ShapeDtypeStruct((users, k), jnp.float32),
            jax.ShapeDtypeStruct((items, k), jnp.float32),
        ],
        scratch_shapes=[pltpu.VMEM((tile, items), jnp.float32)],
        input_output_aliases=aliases,
        compiler_params=pltpu.CompilerParams(dimension_semantics=("arbitrary",)),
    )(*args)


def _gather_kernel(idx_ref, table_ref, out_ref):
    rows = table_ref.shape[0]
    chunk = idx_ref.shape[1]
    onehot = (idx_ref[...] == lax.broadcasted_iota(jnp.int32, (rows, chunk), 0)).astype(
        jnp.bfloat16
    )
    out_ref[...] = _tn(onehot, table_ref[...]).astype(out_ref.dtype)


def onehot_gather(table, idx, chunk=1024):
    rows, k = table.shape
    n = idx.shape[0]
    return pl.pallas_call(
        _gather_kernel,
        grid=(n // chunk,),
        in_specs=[
            pl.BlockSpec((1, chunk), lambda i: (0, i)),
            pl.BlockSpec((rows, k), lambda i: (0, 0)),
        ],
        out_specs=pl.BlockSpec((chunk, k), lambda i: (i, 0)),
        out_shape=jax.ShapeDtypeStruct((n, k), table.dtype),
    )(idx.reshape(1, n), table)


def _scatter_kernel(idx_ref, val_ref, out_ref):
    i = pl.program_id(0)
    rows = out_ref.shape[0]
    chunk = idx_ref.shape[1]
    onehot = (idx_ref[...] == lax.broadcasted_iota(jnp.int32, (rows, chunk), 0)).astype(
        jnp.bfloat16
    )

    @pl.when(i == 0)
    def _():
        out_ref[...] = jnp.zeros_like(out_ref)

    out_ref[...] += jnp.dot(onehot, val_ref[...], preferred_element_type=jnp.float32)


def onehot_scatter_add(idx, values, rows, chunk=1024):
    n, k = values.shape
    return pl.pallas_call(
        _scatter_kernel,
        grid=(n // chunk,),
        in_specs=[
            pl.BlockSpec((1, chunk), lambda i: (0, i)),
            pl.BlockSpec((chunk, k), lambda i: (i, 0)),
        ],
        out_specs=pl.BlockSpec((rows, k), lambda i: (0, 0)),
        out_shape=jax.ShapeDtypeStruct((rows, k), jnp.float32),
        compiler_params=pltpu.CompilerParams(dimension_semantics=("arbitrary",)),
    )(idx.reshape(1, n), values)


def adagrad(current, history, gradient):
    updated = history + gradient * gradient
    return (current - LEARN_RATE * gradient / jnp.sqrt(updated), updated)


def body(
    users,
    user_accum,
    positives,
    hot_table,
    hot_accum,
    cold_table,
    cold_accum,
    cold_requests,
    cold_counts,
):
    user_half = users.astype(jnp.bfloat16)
    hot_half = hot_table.astype(jnp.bfloat16)
    cold_half = cold_table.astype(jnp.bfloat16)
    feature_count = users.shape[1]
    item_sub = hot_table.shape[0]
    sb_count = lax.axis_size("sb")
    pos_count = positives.shape[1]
    devices = cold_requests.shape[1]
    slot_count = cold_requests.shape[2]
    requests = cold_requests.reshape(devices, slot_count)
    live_slots = lax.iota(jnp.int32, slot_count)[None, :] < cold_counts.reshape(devices, 1)
    asked_rows = lax.all_to_all(requests, ("grp", "sa", "sb"), split_axis=0, concat_axis=0, tiled=True)
    found = onehot_gather(cold_half, asked_rows.reshape(-1))
    sub_rows = positives.shape[0] * pos_count // LANES
    packed = jnp.concatenate(
        [
            user_half,
            (positives // LANES).reshape(sub_rows, LANES).astype(jnp.bfloat16),
            (positives % LANES).reshape(sub_rows, LANES).astype(jnp.bfloat16),
        ],
        axis=0,
    )
    packed_part = lax.all_gather(packed, "sb", axis=0, tiled=False)
    hot_part = lax.all_gather(hot_half, "sa", axis=0, tiled=True)
    found, packed_part, hot_part = lax.optimization_barrier((found, packed_part, hot_part))
    fetched = lax.all_to_all(
        found.reshape(devices, slot_count, feature_count),
        ("grp", "sa", "sb"),
        split_axis=0,
        concat_axis=0,
        tiled=True,
    )
    local_users = user_half.shape[0]
    users_part = packed_part[:, :local_users].reshape(-1, feature_count)
    pos_hi = packed_part[:, local_users:local_users + sub_rows].reshape(-1, LANES).astype(jnp.int32)
    pos_lo = packed_part[:, local_users + sub_rows:].reshape(-1, LANES).astype(jnp.int32)
    hi_per_item = item_sub // LANES
    owner = pos_hi // hi_per_item
    local_hi = (owner // sb_count) * hi_per_item + pos_hi % hi_per_item
    pos_hi_t = jnp.where(owner % sb_count == lax.axis_index("sb"), local_hi, hot_part.shape[0] // LANES)
    pos_lo_t = pos_lo
    tiles = users_part.shape[0] // 512
    user_hot_part, item_part = hot_terms(users_part, pos_hi_t, pos_lo_t, hot_part, 0, tiles, found)
    fetched, user_hot_part, item_part = lax.optimization_barrier((fetched, user_hot_part, item_part))
    item_grad = lax.psum_scatter(item_part, ("sa", "grp"), scatter_dimension=0, tiled=True)
    hot_grad = lax.all_gather(item_grad, "grp", axis=0, tiled=True)
    user_hot_part, hot_grad = lax.optimization_barrier((user_hot_part, hot_grad))
    user_hot = lax.psum_scatter(user_hot_part, "sb", scatter_dimension=0, tiled=True)
    flat_rows = fetched.reshape(devices * slot_count, feature_count)
    scores = jnp.einsum("uk,rk->ur", user_half, flat_rows, preferred_element_type=jnp.float32)
    weights = (jax.nn.sigmoid(scores) * live_slots.reshape(1, -1).astype(jnp.float32)).astype(
        jnp.bfloat16
    )
    user_cold = jnp.dot(weights, flat_rows, preferred_element_type=jnp.float32)
    row_terms = jnp.einsum(
        "ur,uk->rk", weights, user_half, preferred_element_type=jnp.float32
    ).astype(jnp.bfloat16)
    row_terms = row_terms.reshape(devices, slot_count, feature_count)
    returned = lax.all_to_all(row_terms, ("grp", "sa", "sb"), split_axis=0, concat_axis=0, tiled=True)
    returned, user_cold = lax.optimization_barrier((returned, user_cold))
    cold_grad = onehot_scatter_add(
        asked_rows.reshape(-1),
        returned.reshape(devices * slot_count, feature_count),
        cold_table.shape[0],
    )
    user_grad = user_hot + user_cold
    new_users, new_user_accum = adagrad(users, user_accum, user_grad)
    new_hot, new_hot_accum = adagrad(hot_table, hot_accum, hot_grad)
    new_cold, new_cold_accum = adagrad(cold_table, cold_accum, cold_grad)
    return (new_users, new_user_accum, new_hot, new_hot_accum, new_cold, new_cold_accum)


def _split_mesh(mesh):
    shard = mesh.shape["shard"]
    sa = 4 if shard % 4 == 0 else 1
    return Mesh(mesh.devices.reshape(mesh.shape["grp"], sa, shard // sa), ("grp", "sa", "sb"))


def solution(mesh):
    return jax.shard_map(
        body,
        mesh=_split_mesh(mesh),
        in_specs=(
            P(("grp", "sa", "sb"), None),
            P(("grp", "sa", "sb"), None),
            P(("grp", "sa", "sb"), None),
            P(("sa", "sb"), None),
            P(("sa", "sb"), None),
            P(("grp", "sa", "sb"), None),
            P(("grp", "sa", "sb"), None),
            P(("grp", "sa", "sb"), None, None),
            P(("grp", "sa", "sb"), None),
        ),
        out_specs=(
            P(("grp", "sa", "sb"), None),
            P(("grp", "sa", "sb"), None),
            P(("sa", "sb"), None),
            P(("sa", "sb"), None),
            P(("grp", "sa", "sb"), None),
            P(("grp", "sa", "sb"), None),
        ),
        check_vma=False,
    )
```

```python
import functools

import jax
import jax.numpy as jnp
from jax import lax
from jax.experimental import pallas as pl
from jax.experimental.pallas import tpu as pltpu
from jax.sharding import Mesh, PartitionSpec as P

POSITIVE_WEIGHT = 32.0
LEARN_RATE = 0.5
LANES = 128
SUB = 8


def _nt(a, b):
    return lax.dot_general(a, b, (((1,), (1,)), ((), ())), preferred_element_type=jnp.float32)


def _tn(a, b):
    return lax.dot_general(a, b, (((0,), (0,)), ((), ())), preferred_element_type=jnp.float32)


def _hot_kernel(u_ref, h_ref, ph_ref, pl_ref, dep_ref, *rest, sub_users, chained):
    del dep_ref
    if chained:
        _, ipin_ref, up_ref, ip_ref, m_ref = rest
    else:
        up_ref, ip_ref, m_ref = rest
    i = pl.program_id(0)
    items = h_ref.shape[0]
    nh = items // LANES
    subtiles = ph_ref.shape[0]
    width = ph_ref.shape[1]
    per = width // sub_users
    r = lax.broadcasted_iota(jnp.int32, (nh * sub_users, width), 0)
    c = lax.broadcasted_iota(jnp.int32, (nh * sub_users, width), 1)
    diag = (r % sub_users) == (c // per)
    hrow = r // sub_users
    lrow = lax.broadcasted_iota(jnp.int32, (LANES, width), 0)

    def sub(s, carry):
        lhs = jnp.where(diag & (ph_ref[pl.ds(s, 1), :] == hrow), 1.0, 0.0).astype(jnp.bfloat16)
        rhs = jnp.where(pl_ref[pl.ds(s, 1), :] == lrow, 1.0, 0.0).astype(jnp.bfloat16)
        out = _nt(lhs, rhs)
        base = pl.multiple_of(s * sub_users, sub_users)
        for h in range(nh):
            m_ref[pl.ds(base, sub_users), pl.ds(h * LANES, LANES)] = out[
                h * sub_users:(h + 1) * sub_users, :
            ]
        return carry

    lax.fori_loop(0, subtiles, sub, 0, unroll=subtiles)
    u = u_ref[...]
    hj = h_ref[...]
    scores = _nt(u, hj)
    m = m_ref[...]
    w = ((1.0 + POSITIVE_WEIGHT * m) * jax.nn.sigmoid(scores) - POSITIVE_WEIGHT * m).astype(
        jnp.bfloat16
    )
    up_ref[...] = jnp.dot(w, hj, preferred_element_type=jnp.float32)

    @pl.when(i == 0)
    def _():
        if chained:
            ip_ref[...] = ipin_ref[...]
        else:
            ip_ref[...] = jnp.zeros_like(ip_ref)

    ip_ref[...] += _tn(w, u)


def hot_prepare(positives, sub_users=8):
    users, pos_count = positives.shape
    subtiles = users // sub_users
    width = sub_users * pos_count
    return (
        (positives // LANES).reshape(subtiles, width),
        (positives % LANES).reshape(subtiles, width),
    )


def hot_terms(user_half, pos_hi, pos_lo, hot_rows, first, count, dep, prev=None, tile=512, sub_users=8):
    users, k = user_half.shape
    items = hot_rows.shape[0]
    width = pos_hi.shape[1]
    per_tile = tile // sub_users
    in_specs = [
        pl.BlockSpec((tile, k), lambda i: (first + i, 0)),
        pl.BlockSpec((items, k), lambda i: (0, 0)),
        pl.BlockSpec((per_tile, width), lambda i: (first + i, 0)),
        pl.BlockSpec((per_tile, width), lambda i: (first + i, 0)),
        pl.BlockSpec(memory_space=pl.ANY),
    ]
    args = [user_half, hot_rows, pos_hi, pos_lo, dep]
    aliases = {}
    if prev is not None:
        in_specs += [pl.BlockSpec(memory_space=pl.ANY), pl.BlockSpec((items, k), lambda i: (0, 0))]
        args += list(prev)
        aliases = {5: 0, 6: 1}
    return pl.pallas_call(
        functools.partial(_hot_kernel, sub_users=sub_users, chained=prev is not None),
        grid=(count,),
        in_specs=in_specs,
        out_specs=[
            pl.BlockSpec((tile, k), lambda i: (first + i, 0)),
            pl.BlockSpec((items, k), lambda i: (0, 0)),
        ],
        out_shape=[
            jax.ShapeDtypeStruct((users, k), jnp.float32),
            jax.ShapeDtypeStruct((items, k), jnp.float32),
        ],
        scratch_shapes=[pltpu.VMEM((tile, items), jnp.float32)],
        input_output_aliases=aliases,
        compiler_params=pltpu.CompilerParams(dimension_semantics=("arbitrary",)),
    )(*args)


def _gather_kernel(idx_ref, table_ref, out_ref):
    rows = table_ref.shape[0]
    chunk = idx_ref.shape[1]
    onehot = (idx_ref[...] == lax.broadcasted_iota(jnp.int32, (rows, chunk), 0)).astype(
        jnp.bfloat16
    )
    out_ref[...] = _tn(onehot, table_ref[...]).astype(out_ref.dtype)


def onehot_gather(table, idx, chunk=1024):
    rows, k = table.shape
    n = idx.shape[0]
    return pl.pallas_call(
        _gather_kernel,
        grid=(n // chunk,),
        in_specs=[
            pl.BlockSpec((1, chunk), lambda i: (0, i)),
            pl.BlockSpec((rows, k), lambda i: (0, 0)),
        ],
        out_specs=pl.BlockSpec((chunk, k), lambda i: (i, 0)),
        out_shape=jax.ShapeDtypeStruct((n, k), table.dtype),
    )(idx.reshape(1, n), table)


def _scatter_kernel(idx_ref, val_ref, out_ref):
    i = pl.program_id(0)
    rows = out_ref.shape[0]
    chunk = idx_ref.shape[1]
    onehot = (idx_ref[...] == lax.broadcasted_iota(jnp.int32, (rows, chunk), 0)).astype(
        jnp.bfloat16
    )

    @pl.when(i == 0)
    def _():
        out_ref[...] = jnp.zeros_like(out_ref)

    out_ref[...] += jnp.dot(onehot, val_ref[...], preferred_element_type=jnp.float32)


def onehot_scatter_add(idx, values, rows, chunk=1024):
    n, k = values.shape
    return pl.pallas_call(
        _scatter_kernel,
        grid=(n // chunk,),
        in_specs=[
            pl.BlockSpec((1, chunk), lambda i: (0, i)),
            pl.BlockSpec((chunk, k), lambda i: (i, 0)),
        ],
        out_specs=pl.BlockSpec((rows, k), lambda i: (0, 0)),
        out_shape=jax.ShapeDtypeStruct((rows, k), jnp.float32),
        compiler_params=pltpu.CompilerParams(dimension_semantics=("arbitrary",)),
    )(idx.reshape(1, n), values)


def adagrad(current, history, gradient):
    updated = history + gradient * gradient
    return (current - LEARN_RATE * gradient / jnp.sqrt(updated), updated)


def body(
    users,
    user_accum,
    positives,
    hot_table,
    hot_accum,
    cold_table,
    cold_accum,
    cold_requests,
    cold_counts,
):
    user_half = users.astype(jnp.bfloat16)
    hot_half = hot_table.astype(jnp.bfloat16)
    cold_half = cold_table.astype(jnp.bfloat16)
    feature_count = users.shape[1]
    item_sub = hot_table.shape[0]
    sb_count = lax.axis_size("sb")
    pos_count = positives.shape[1]
    devices = cold_requests.shape[1]
    slot_count = cold_requests.shape[2]
    requests = cold_requests.reshape(devices, slot_count)
    live_slots = lax.iota(jnp.int32, slot_count)[None, :] < cold_counts.reshape(devices, 1)
    asked_rows = lax.all_to_all(requests, ("grp", "sa", "sb"), split_axis=0, concat_axis=0, tiled=True)
    found = onehot_gather(cold_half, asked_rows.reshape(-1))
    sub_rows = positives.shape[0] * pos_count // LANES
    packed = jnp.concatenate(
        [
            user_half,
            (positives // LANES).reshape(sub_rows, LANES).astype(jnp.bfloat16),
            (positives % LANES).reshape(sub_rows, LANES).astype(jnp.bfloat16),
        ],
        axis=0,
    )
    packed_part = lax.all_gather(packed, "sb", axis=0, tiled=False)
    hot_part = lax.all_gather(hot_half, "sa", axis=0, tiled=True)
    found, packed_part, hot_part = lax.optimization_barrier((found, packed_part, hot_part))
    fetched = lax.all_to_all(
        found.reshape(devices, slot_count, feature_count),
        ("grp", "sa", "sb"),
        split_axis=0,
        concat_axis=0,
        tiled=True,
    )
    local_users = user_half.shape[0]
    users_part = packed_part[:, :local_users].reshape(-1, feature_count)
    pos_hi = packed_part[:, local_users:local_users + sub_rows].reshape(-1, LANES).astype(jnp.int32)
    pos_lo = packed_part[:, local_users + sub_rows:].reshape(-1, LANES).astype(jnp.int32)
    hi_per_item = item_sub // LANES
    owner = pos_hi // hi_per_item
    local_hi = (owner // sb_count) * hi_per_item + pos_hi % hi_per_item
    pos_hi_t = jnp.where(owner % sb_count == lax.axis_index("sb"), local_hi, hot_part.shape[0] // LANES)
    pos_lo_t = pos_lo
    tiles = users_part.shape[0] // 512
    user_hot_part, item_part = hot_terms(users_part, pos_hi_t, pos_lo_t, hot_part, 0, tiles, found)
    fetched, user_hot_part, item_part = lax.optimization_barrier((fetched, user_hot_part, item_part))
    item_grad = lax.psum_scatter(item_part, "sa", scatter_dimension=0, tiled=True)
    user_hot = lax.psum_scatter(user_hot_part, "sb", scatter_dimension=0, tiled=True)
    flat_rows = fetched.reshape(devices * slot_count, feature_count)
    scores = jnp.einsum("uk,rk->ur", user_half, flat_rows, preferred_element_type=jnp.float32)
    weights = (jax.nn.sigmoid(scores) * live_slots.reshape(1, -1).astype(jnp.float32)).astype(
        jnp.bfloat16
    )
    user_cold = jnp.dot(weights, flat_rows, preferred_element_type=jnp.float32)
    row_terms = jnp.einsum(
        "ur,uk->rk", weights, user_half, preferred_element_type=jnp.float32
    ).astype(jnp.bfloat16)
    row_terms = row_terms.reshape(devices, slot_count, feature_count)
    returned = lax.all_to_all(row_terms, ("grp", "sa", "sb"), split_axis=0, concat_axis=0, tiled=True)
    returned, user_cold, item_grad, user_hot = lax.optimization_barrier(
        (returned, user_cold, item_grad, user_hot)
    )
    hot_grad = lax.psum(item_grad, "grp")
    cold_grad = onehot_scatter_add(
        asked_rows.reshape(-1),
        returned.reshape(devices * slot_count, feature_count),
        cold_table.shape[0],
    )
    user_grad = user_hot + user_cold
    new_users, new_user_accum = adagrad(users, user_accum, user_grad)
    new_hot, new_hot_accum = adagrad(hot_table, hot_accum, hot_grad)
    new_cold, new_cold_accum = adagrad(cold_table, cold_accum, cold_grad)
    return (new_users, new_user_accum, new_hot, new_hot_accum, new_cold, new_cold_accum)


def _split_mesh(mesh):
    shard = mesh.shape["shard"]
    sa = 4 if shard % 4 == 0 else 1
    return Mesh(mesh.devices.reshape(mesh.shape["grp"], sa, shard // sa), ("grp", "sa", "sb"))


def solution(mesh):
    return jax.shard_map(
        body,
        mesh=_split_mesh(mesh),
        in_specs=(
            P(("grp", "sa", "sb"), None),
            P(("grp", "sa", "sb"), None),
            P(("grp", "sa", "sb"), None),
            P(("sa", "sb"), None),
            P(("sa", "sb"), None),
            P(("grp", "sa", "sb"), None),
            P(("grp", "sa", "sb"), None),
            P(("grp", "sa", "sb"), None, None),
            P(("grp", "sa", "sb"), None),
        ),
        out_specs=(
            P(("grp", "sa", "sb"), None),
            P(("grp", "sa", "sb"), None),
            P(("sa", "sb"), None),
            P(("sa", "sb"), None),
            P(("grp", "sa", "sb"), None),
            P(("grp", "sa", "sb"), None),
        ),
        check_vma=False,
    )
```

```python
import functools

import jax
import jax.numpy as jnp
from jax import lax
from jax.experimental import pallas as pl
from jax.experimental.pallas import tpu as pltpu
from jax.sharding import Mesh, PartitionSpec as P

POSITIVE_WEIGHT = 32.0
LEARN_RATE = 0.5
LANES = 128
SUB = 8


def _nt(a, b):
    return lax.dot_general(a, b, (((1,), (1,)), ((), ())), preferred_element_type=jnp.float32)


def _tn(a, b):
    return lax.dot_general(a, b, (((0,), (0,)), ((), ())), preferred_element_type=jnp.float32)


def _hot_kernel(u_ref, h_ref, ph_ref, pl_ref, dep_ref, *rest, sub_users, chained):
    del dep_ref
    if chained:
        _, ipin_ref, up_ref, ip_ref, m_ref = rest
    else:
        up_ref, ip_ref, m_ref = rest
    i = pl.program_id(0)
    items = h_ref.shape[0]
    nh = items // LANES
    subtiles = ph_ref.shape[0]
    width = ph_ref.shape[1]
    per = width // sub_users
    r = lax.broadcasted_iota(jnp.int32, (nh * sub_users, width), 0)
    c = lax.broadcasted_iota(jnp.int32, (nh * sub_users, width), 1)
    diag = (r % sub_users) == (c // per)
    hrow = r // sub_users
    lrow = lax.broadcasted_iota(jnp.int32, (LANES, width), 0)

    def sub(s, carry):
        lhs = jnp.where(diag & (ph_ref[pl.ds(s, 1), :] == hrow), 1.0, 0.0).astype(jnp.bfloat16)
        rhs = jnp.where(pl_ref[pl.ds(s, 1), :] == lrow, 1.0, 0.0).astype(jnp.bfloat16)
        out = _nt(lhs, rhs)
        base = pl.multiple_of(s * sub_users, sub_users)
        for h in range(nh):
            m_ref[pl.ds(base, sub_users), pl.ds(h * LANES, LANES)] = out[
                h * sub_users:(h + 1) * sub_users, :
            ]
        return carry

    lax.fori_loop(0, subtiles, sub, 0, unroll=subtiles)
    u = u_ref[...]
    hj = h_ref[...]
    scores = _nt(u, hj)
    m = m_ref[...]
    w = ((1.0 + POSITIVE_WEIGHT * m) * jax.nn.sigmoid(scores) - POSITIVE_WEIGHT * m).astype(
        jnp.bfloat16
    )
    up_ref[...] = jnp.dot(w, hj, preferred_element_type=jnp.float32)

    @pl.when(i == 0)
    def _():
        if chained:
            ip_ref[...] = ipin_ref[...]
        else:
            ip_ref[...] = jnp.zeros_like(ip_ref)

    ip_ref[...] += _tn(w, u)


def hot_prepare(positives, sub_users=8):
    users, pos_count = positives.shape
    subtiles = users // sub_users
    width = sub_users * pos_count
    return (
        (positives // LANES).reshape(subtiles, width),
        (positives % LANES).reshape(subtiles, width),
    )


def hot_terms(user_half, pos_hi, pos_lo, hot_rows, first, count, dep, prev=None, tile=512, sub_users=8):
    users, k = user_half.shape
    items = hot_rows.shape[0]
    width = pos_hi.shape[1]
    per_tile = tile // sub_users
    in_specs = [
        pl.BlockSpec((tile, k), lambda i: (first + i, 0)),
        pl.BlockSpec((items, k), lambda i: (0, 0)),
        pl.BlockSpec((per_tile, width), lambda i: (first + i, 0)),
        pl.BlockSpec((per_tile, width), lambda i: (first + i, 0)),
        pl.BlockSpec(memory_space=pl.ANY),
    ]
    args = [user_half, hot_rows, pos_hi, pos_lo, dep]
    aliases = {}
    if prev is not None:
        in_specs += [pl.BlockSpec(memory_space=pl.ANY), pl.BlockSpec((items, k), lambda i: (0, 0))]
        args += list(prev)
        aliases = {5: 0, 6: 1}
    return pl.pallas_call(
        functools.partial(_hot_kernel, sub_users=sub_users, chained=prev is not None),
        grid=(count,),
        in_specs=in_specs,
        out_specs=[
            pl.BlockSpec((tile, k), lambda i: (first + i, 0)),
            pl.BlockSpec((items, k), lambda i: (0, 0)),
        ],
        out_shape=[
            jax.ShapeDtypeStruct((users, k), jnp.float32),
            jax.ShapeDtypeStruct((items, k), jnp.float32),
        ],
        scratch_shapes=[pltpu.VMEM((tile, items), jnp.float32)],
        input_output_aliases=aliases,
        compiler_params=pltpu.CompilerParams(dimension_semantics=("arbitrary",)),
    )(*args)


def _gather_kernel(idx_ref, table_ref, out_ref):
    rows = table_ref.shape[0]
    chunk = idx_ref.shape[1]
    onehot = (idx_ref[...] == lax.broadcasted_iota(jnp.int32, (rows, chunk), 0)).astype(
        jnp.bfloat16
    )
    out_ref[...] = _tn(onehot, table_ref[...]).astype(out_ref.dtype)


def onehot_gather(table, idx, chunk=1024):
    rows, k = table.shape
    n = idx.shape[0]
    return pl.pallas_call(
        _gather_kernel,
        grid=(n // chunk,),
        in_specs=[
            pl.BlockSpec((1, chunk), lambda i: (0, i)),
            pl.BlockSpec((rows, k), lambda i: (0, 0)),
        ],
        out_specs=pl.BlockSpec((chunk, k), lambda i: (i, 0)),
        out_shape=jax.ShapeDtypeStruct((n, k), table.dtype),
    )(idx.reshape(1, n), table)


def _scatter_kernel(idx_ref, val_ref, out_ref):
    i = pl.program_id(0)
    rows = out_ref.shape[0]
    chunk = idx_ref.shape[1]
    onehot = (idx_ref[...] == lax.broadcasted_iota(jnp.int32, (rows, chunk), 0)).astype(
        jnp.bfloat16
    )

    @pl.when(i == 0)
    def _():
        out_ref[...] = jnp.zeros_like(out_ref)

    out_ref[...] += jnp.dot(onehot, val_ref[...], preferred_element_type=jnp.float32)


def onehot_scatter_add(idx, values, rows, chunk=4096):
    n, k = values.shape
    return pl.pallas_call(
        _scatter_kernel,
        grid=(n // chunk,),
        in_specs=[
            pl.BlockSpec((1, chunk), lambda i: (0, i)),
            pl.BlockSpec((chunk, k), lambda i: (i, 0)),
        ],
        out_specs=pl.BlockSpec((rows, k), lambda i: (0, 0)),
        out_shape=jax.ShapeDtypeStruct((rows, k), jnp.float32),
        compiler_params=pltpu.CompilerParams(dimension_semantics=("arbitrary",)),
    )(idx.reshape(1, n), values)


def adagrad(current, history, gradient):
    updated = history + gradient * gradient
    return (current - LEARN_RATE * gradient / jnp.sqrt(updated), updated)


def body(
    users,
    user_accum,
    positives,
    hot_table,
    hot_accum,
    cold_table,
    cold_accum,
    cold_requests,
    cold_counts,
):
    user_half = users.astype(jnp.bfloat16)
    hot_half = hot_table.astype(jnp.bfloat16)
    cold_half = cold_table.astype(jnp.bfloat16)
    feature_count = users.shape[1]
    item_sub = hot_table.shape[0]
    sb_count = lax.axis_size("sb")
    pos_count = positives.shape[1]
    devices = cold_requests.shape[1]
    slot_count = cold_requests.shape[2]
    requests = cold_requests.reshape(devices, slot_count)
    live_slots = lax.iota(jnp.int32, slot_count)[None, :] < cold_counts.reshape(devices, 1)
    asked_rows = lax.all_to_all(requests, ("grp", "sa", "sb"), split_axis=0, concat_axis=0, tiled=True)
    found = onehot_gather(cold_half, asked_rows.reshape(-1))
    sub_rows = positives.shape[0] * pos_count // LANES
    packed = jnp.concatenate(
        [
            user_half,
            (positives // LANES).reshape(sub_rows, LANES).astype(jnp.bfloat16),
            (positives % LANES).reshape(sub_rows, LANES).astype(jnp.bfloat16),
        ],
        axis=0,
    )
    packed_part = lax.all_gather(packed, "sb", axis=0, tiled=False)
    hot_part = lax.all_gather(hot_half, "sa", axis=0, tiled=True)
    found, packed_part, hot_part = lax.optimization_barrier((found, packed_part, hot_part))
    fetched = lax.all_to_all(
        found.reshape(devices, slot_count, feature_count),
        ("grp", "sa", "sb"),
        split_axis=0,
        concat_axis=0,
        tiled=True,
    )
    local_users = user_half.shape[0]
    users_part = packed_part[:, :local_users].reshape(-1, feature_count)
    pos_hi = packed_part[:, local_users:local_users + sub_rows].reshape(-1, LANES).astype(jnp.int32)
    pos_lo = packed_part[:, local_users + sub_rows:].reshape(-1, LANES).astype(jnp.int32)
    hi_per_item = item_sub // LANES
    owner = pos_hi // hi_per_item
    local_hi = (owner // sb_count) * hi_per_item + pos_hi % hi_per_item
    pos_hi_t = jnp.where(owner % sb_count == lax.axis_index("sb"), local_hi, hot_part.shape[0] // LANES)
    pos_lo_t = pos_lo
    tiles = users_part.shape[0] // 512
    user_hot_part, item_part = hot_terms(users_part, pos_hi_t, pos_lo_t, hot_part, 0, tiles, found)
    fetched, user_hot_part, item_part = lax.optimization_barrier((fetched, user_hot_part, item_part))
    item_grad = lax.psum_scatter(item_part, "sa", scatter_dimension=0, tiled=True)
    user_hot = lax.psum_scatter(user_hot_part, "sb", scatter_dimension=0, tiled=True)
    flat_rows = fetched.reshape(devices * slot_count, feature_count)
    scores = jnp.einsum("uk,rk->ur", user_half, flat_rows, preferred_element_type=jnp.float32)
    weights = (jax.nn.sigmoid(scores) * live_slots.reshape(1, -1).astype(jnp.float32)).astype(
        jnp.bfloat16
    )
    user_cold = jnp.dot(weights, flat_rows, preferred_element_type=jnp.float32)
    row_terms = jnp.einsum(
        "ur,uk->rk", weights, user_half, preferred_element_type=jnp.float32
    ).astype(jnp.bfloat16)
    row_terms = row_terms.reshape(devices, slot_count, feature_count)
    returned = lax.all_to_all(row_terms, ("grp", "sa", "sb"), split_axis=0, concat_axis=0, tiled=True)
    returned, user_cold, item_grad, user_hot = lax.optimization_barrier(
        (returned, user_cold, item_grad, user_hot)
    )
    hot_grad = lax.psum(item_grad, "grp")
    cold_grad = onehot_scatter_add(
        asked_rows.reshape(-1),
        returned.reshape(devices * slot_count, feature_count),
        cold_table.shape[0],
    )
    user_grad = user_hot + user_cold
    new_users, new_user_accum = adagrad(users, user_accum, user_grad)
    new_hot, new_hot_accum = adagrad(hot_table, hot_accum, hot_grad)
    new_cold, new_cold_accum = adagrad(cold_table, cold_accum, cold_grad)
    return (new_users, new_user_accum, new_hot, new_hot_accum, new_cold, new_cold_accum)


def _split_mesh(mesh):
    shard = mesh.shape["shard"]
    sa = 4 if shard % 4 == 0 else 1
    return Mesh(mesh.devices.reshape(mesh.shape["grp"], sa, shard // sa), ("grp", "sa", "sb"))


def solution(mesh):
    return jax.shard_map(
        body,
        mesh=_split_mesh(mesh),
        in_specs=(
            P(("grp", "sa", "sb"), None),
            P(("grp", "sa", "sb"), None),
            P(("grp", "sa", "sb"), None),
            P(("sa", "sb"), None),
            P(("sa", "sb"), None),
            P(("grp", "sa", "sb"), None),
            P(("grp", "sa", "sb"), None),
            P(("grp", "sa", "sb"), None, None),
            P(("grp", "sa", "sb"), None),
        ),
        out_specs=(
            P(("grp", "sa", "sb"), None),
            P(("grp", "sa", "sb"), None),
            P(("sa", "sb"), None),
            P(("sa", "sb"), None),
            P(("grp", "sa", "sb"), None),
            P(("grp", "sa", "sb"), None),
        ),
        check_vma=False,
    )
```
